128 devices in a mesh: dp: 8 (over y, z_hi), fsdp: 16 (over x, z_lo, core).
Axes of the slice: x: 4, y: 4, z: 4 (z_hi: 2, z_lo: 2; z = z_hi * 2 + z_lo), core: 2. Of those that a mesh axis runs over, the one named last changes fastest.
Arguments:
- x_src: bfloat16 [512, 8192], P('fsdp', 'dp'), may hold values from -6 to 6
- doc_lengths: int32 [16, 4], replicated, may hold values from 1 to 16, as said below
- doc_dests: int32 [16, 4], replicated, may hold values from 0 to 15, as said below
- w_gate: bfloat16 [8192, 14336], P('dp', 'fsdp'), may hold values from -0.0625 to 0.0625
- w_up: bfloat16 [8192, 14336], P('dp', 'fsdp'), may hold values from -0.0625 to 0.0625
- w_down: bfloat16 [14336, 8192], P('fsdp', 'dp'), may hold values from -0.046875 to 0.046875
- basis: float32 [8192, 512], P('dp'), may hold values from -0.0625 to 0.0625
- out_cotangent: bfloat16 [1024, 8192], P('fsdp', 'dp'), may hold values from -6 to 6
Outputs:
- layer_out: bfloat16 [1024, 8192], P('fsdp', 'dp')
- input_grad: bfloat16 [1024, 8192], P('fsdp', 'dp')
- grad_gate: float32 [8192, 14336], P('dp', 'fsdp')
- grad_up: float32 [8192, 14336], P('dp', 'fsdp')
- grad_down: float32 [14336, 8192], P('fsdp', 'dp')
The draws below stay inside these ranges and needn't reach their ends.
Inputs may be any that keep to these rules, and one draw needn't show every extreme that they name: `doc_lengths`: the 4 lengths of a source sum to 32 and one of them equals 16. `doc_dests`: document c of every source s goes to destination (s + o_c) modulo 16, for 4 different offsets o_c shared by all sources, one of which is 8; a destination receives at most 64 tokens in all, and some destination receives exactly 64.
All inputs are finite; a program needn't handle non-finite values.
Results may differ from the reference program's by a relative error of at most 0.034.
Values may be sent and summed in bfloat16 or wider, within the bound.
No kernel may reach another device: no remote copies, remote signals or barrier semaphores. Data moves between devices by JAX's collectives and lax.ppermute only.
A program may use at most 128 MiB of HBM per device.

```python
import jax
import jax.numpy as jnp
from jax import lax

D = 8192
FW = 14336
KEYS = 512
TOK_SRC = 32
NDOC = 4
MOST = 16
RECV = 64
SOURCES = 16
N_DP = 8
N_FSDP = 16


def deal_plan(key):
    base = jax.random.fold_in(key, 7)
    keys_all = jax.random.split(base, 6)
    half = SOURCES // 2
    others = jax.random.permutation(keys_all[0], SOURCES - 1)[:NDOC - 1].astype(jnp.int32)
    others = others + (others >= half).astype(jnp.int32)
    shifts = jnp.concatenate([jnp.full((1,), half, jnp.int32), others])
    order = jax.random.permutation(keys_all[5], NDOC).astype(jnp.int32)
    shifts = jnp.take(shifts, order).astype(jnp.int32)
    sources = jnp.arange(SOURCES, dtype=jnp.int32)
    dests = (sources[:, None] + shifts[None, :]) % SOURCES
    root = jax.random.randint(keys_all[1], (), 0, SOURCES).astype(jnp.int32)
    longpos = jax.random.randint(keys_all[2], (SOURCES,), 0, NDOC).astype(jnp.int32)
    special = (root - shifts) % SOURCES
    match = (sources[:, None] == special[None, :]).astype(jnp.int32)
    docs = jnp.arange(NDOC, dtype=jnp.int32)
    forced = jnp.sum(match * docs[None, :], axis=1)
    longpos = jnp.where(jnp.sum(match, axis=1) > 0, forced, longpos)
    first_cut = jax.random.randint(keys_all[3], (SOURCES,), 1, MOST).astype(jnp.int32)
    second_cut = jax.random.randint(keys_all[4], (SOURCES,), 1, MOST - 1).astype(jnp.int32)
    second_cut = second_cut + (second_cut >= first_cut).astype(jnp.int32)
    lower = jnp.minimum(first_cut, second_cut)
    upper = jnp.maximum(first_cut, second_cut)
    parts = jnp.stack([lower, upper - lower, MOST - upper], axis=1)
    rank = docs[None, :] - (docs[None, :] > longpos[:, None]).astype(jnp.int32)
    rank = jnp.clip(rank, 0, 2)
    picked = jnp.take_along_axis(parts, rank, axis=1)
    lengths = jnp.where(docs[None, :] == longpos[:, None], MOST, picked)
    return (lengths.astype(jnp.int32), dests.astype(jnp.int32))


def draw_doc_lengths(key, part):
    return deal_plan(key)[0]


def draw_doc_dests(key, part):
    return deal_plan(key)[1]


def steps_of(stream_key, extent, cuts, least, largest):
    level = 1.0
    for position, shards_of in cuts:
        heights = jax.random.uniform(jax.random.fold_in(jax.random.fold_in(stream_key, 6), position), (shards_of,), jnp.float32, least / len(cuts), largest / len(cuts))
        level = level * jnp.repeat(jnp.exp(heights), extent[position] // shards_of).reshape((-1,) + (1,) * (len(extent) - 1 - position))
    return level


def noise(own_key, shape, deviation, bound, shards=(), kind=jnp.bfloat16):
    result = deviation * jax.random.normal(own_key, shape, jnp.float32)
    if shards:
        result = result * steps_of(own_key, shape, shards, -0.22, 0.18)
    return jnp.clip(result, -bound, bound).astype(kind)


def setup_inputs(seed: int = 0) -> dict:
    key_of = jax.random.split(jax.random.key(seed), 9)
    x_src = noise(key_of[0], (SOURCES * TOK_SRC, D), 1.0, 6.0, ((0, 16), (1, 8)))
    doc_lengths = draw_doc_lengths(jax.random.fold_in(key_of[8], 71), 0)
    doc_dests = draw_doc_dests(jax.random.fold_in(key_of[8], 71), 0)
    w_gate = noise(key_of[3], (D, FW), D ** -0.5, 0.0625, ((0, 8), (1, 16)))
    w_up = noise(key_of[4], (D, FW), D ** -0.5, 0.0625, ((0, 8), (1, 16)))
    w_down = noise(key_of[5], (FW, D), FW ** -0.5, 0.046875, ((0, 16), (1, 8)))
    basis = noise(key_of[6], (D, KEYS), D ** -0.5, 0.0625, ((0, 8),), jnp.float32)
    out_cotangent = noise(key_of[7], (SOURCES * RECV, D), 1.0, 6.0, ((0, 16), (1, 8)))
    return dict(x_src=x_src, doc_lengths=doc_lengths, doc_dests=doc_dests, w_gate=w_gate, w_up=w_up, w_down=w_down, basis=basis, out_cotangent=out_cotangent)


def deal_tables(doc_lengths, doc_dests):
    starts = (jnp.cumsum(doc_lengths, axis=1) - doc_lengths).astype(jnp.int32)
    targets = jnp.arange(SOURCES, dtype=jnp.int32)
    hits = (doc_dests[:, :, None] == targets[None, None, :]).astype(jnp.int32)
    loads = jnp.sum(doc_lengths[:, :, None] * hits, axis=1).astype(jnp.int32)
    firsts = jnp.sum(starts[:, :, None] * hits, axis=1).astype(jnp.int32)
    return loads, firsts


def settle(term):
    return lax.optimization_barrier(term.astype(jnp.bfloat16)).astype(jnp.float32)


def split_sum(parts, term, shape):
    def step(k, total):
        return total + settle(term(k))
    return lax.fori_loop(0, parts, step, jnp.zeros(shape, jnp.float32))


def reference(x_src, doc_lengths, doc_dests, w_gate, w_up, w_down, basis, out_cotangent):
    loads, firsts = deal_tables(doc_lengths, doc_dests)
    offsets = (jnp.cumsum(loads, axis=0) - loads).astype(jnp.int32)
    ends = offsets + loads
    place = jnp.arange(RECV, dtype=jnp.int32)
    owner = jnp.sum((ends[:, :, None] <= place[None, None, :]).astype(jnp.int32), axis=0)
    owner = jnp.minimum(owner, SOURCES - 1)
    pick = (owner[None, :, :] == jnp.arange(SOURCES, dtype=jnp.int32)[:, None, None]).astype(jnp.int32)
    own_offset = jnp.sum(pick * offsets[:, :, None], axis=0)
    own_first = jnp.sum(pick * firsts[:, :, None], axis=0)
    valid = place[None, :] < jnp.sum(loads, axis=0)[:, None]
    index = owner * TOK_SRC + own_first + place[None, :] - own_offset
    index = jnp.where(valid, index, 0).astype(jnp.int32).reshape(-1)
    dealt = jnp.take(x_src, index, axis=0)
    dealt = jnp.where(valid.reshape(-1)[:, None], dealt, jnp.zeros_like(dealt))
    rows = dealt.shape[0]
    feat = D // N_DP
    unit = FW // N_FSDP
    contract_cols = (((1,), (1,)), ((), ()))

    def gate_term(k):
        start = (k * feat).astype(jnp.int32)
        block = lax.dynamic_slice_in_dim(dealt, start, feat, 1)
        return jnp.dot(block, lax.dynamic_slice_in_dim(w_gate, start, feat, 0), preferred_element_type=jnp.float32)

    def up_term(k):
        start = (k * feat).astype(jnp.int32)
        block = lax.dynamic_slice_in_dim(dealt, start, feat, 1)
        return jnp.dot(block, lax.dynamic_slice_in_dim(w_up, start, feat, 0), preferred_element_type=jnp.float32)

    gate = split_sum(N_DP, gate_term, (rows, FW))
    up = split_sum(N_DP, up_term, (rows, FW))
    hidden = (jax.nn.silu(gate) * up).astype(jnp.bfloat16)

    def out_term(j):
        start = (j * unit).astype(jnp.int32)
        block = lax.dynamic_slice_in_dim(hidden, start, unit, 1)
        return jnp.dot(block, lax.dynamic_slice_in_dim(w_down, start, unit, 0), preferred_element_type=jnp.float32)

    layer_out = split_sum(N_FSDP, out_term, (rows, D)).astype(jnp.bfloat16)

    def hgrad_term(k):
        start = (k * feat).astype(jnp.int32)
        block = lax.dynamic_slice_in_dim(out_cotangent, start, feat, 1)
        wpart = lax.dynamic_slice_in_dim(w_down, start, feat, 1)
        return lax.dot_general(block, wpart, contract_cols, preferred_element_type=jnp.float32)

    hidden_grad = split_sum(N_DP, hgrad_term, (rows, FW))
    sig = jax.nn.sigmoid(gate)
    gate_grad = (hidden_grad * up * sig * (1.0 + gate * (1.0 - sig))).astype(jnp.bfloat16)
    up_grad = (hidden_grad * gate * sig).astype(jnp.bfloat16)
    grad_down = lax.dot_general(hidden, out_cotangent, (((0,), (0,)), ((), ())), preferred_element_type=jnp.float32)
    raw_gate = lax.dot_general(dealt, gate_grad, (((0,), (0,)), ((), ())), preferred_element_type=jnp.float32)
    raw_up = lax.dot_general(dealt, up_grad, (((0,), (0,)), ((), ())), preferred_element_type=jnp.float32)
    high = lax.Precision.HIGHEST
    over_gate = lax.dot_general(basis, raw_gate, (((0,), (0,)), ((), ())), precision=high)
    grad_gate = raw_gate - jnp.dot(basis, over_gate, precision=high)
    over_up = lax.dot_general(basis, raw_up, (((0,), (0,)), ((), ())), precision=high)
    grad_up = raw_up - jnp.dot(basis, over_up, precision=high)

    def in_term(j):
        start = (j * unit).astype(jnp.int32)
        first = lax.dot_general(lax.dynamic_slice_in_dim(gate_grad, start, unit, 1), lax.dynamic_slice_in_dim(w_gate, start, unit, 1), contract_cols, preferred_element_type=jnp.float32)
        second = lax.dot_general(lax.dynamic_slice_in_dim(up_grad, start, unit, 1), lax.dynamic_slice_in_dim(w_up, start, unit, 1), contract_cols, preferred_element_type=jnp.float32)
        return first + second

    input_grad = split_sum(N_FSDP, in_term, (rows, D)).astype(jnp.bfloat16)
    return layer_out, input_grad, grad_gate, grad_up, grad_down
```

```python
import jax
import jax.numpy as jnp
from jax import lax
from jax.sharding import PartitionSpec as P

MOST = 16


def deal_tables(doc_lengths, doc_dests):
    groups = doc_lengths.shape[0]
    starts = jnp.cumsum(doc_lengths, axis=1) - doc_lengths
    targets = jnp.arange(groups, dtype=jnp.int32)
    hits = (doc_dests[:, :, None] == targets[None, None, :]).astype(jnp.int32)
    loads = jnp.sum(doc_lengths[:, :, None] * hits, axis=1)
    firsts = jnp.sum(starts[:, :, None] * hits, axis=1)
    return (loads, firsts)


def token_rows(doc_lengths, doc_dests, loads, tok, recv):
    starts = jnp.cumsum(doc_lengths, axis=1) - doc_lengths
    ends = starts + doc_lengths
    offsets = jnp.cumsum(loads, axis=0) - loads
    t = jnp.arange(tok, dtype=jnp.int32)
    doc_of = jnp.sum((ends[:, :, None] <= t[None, None, :]).astype(jnp.int32), axis=1)
    doc_of = jnp.minimum(doc_of, doc_lengths.shape[1] - 1)
    dst = jnp.take_along_axis(doc_dests, doc_of, axis=1)
    st = jnp.take_along_axis(starts, doc_of, axis=1)
    off = jnp.take_along_axis(offsets, dst, axis=1)
    row = dst * recv + off + t[None, :] - st
    return jnp.clip(row, 0, loads.shape[0] * recv - 1).reshape(-1)


def settle(term):
    return lax.optimization_barrier(term.astype(jnp.bfloat16)).astype(jnp.float32)


def pack_slots(rows, loads_out, firsts_out, depth):
    inner = jnp.arange(depth, dtype=jnp.int32)
    valid = inner[None, :] < loads_out[:, None]
    index = jnp.where(valid, firsts_out[:, None] + inner[None, :], 0).reshape(-1)
    taken = jnp.take(rows, index, axis=0).reshape(loads_out.shape[0], depth, rows.shape[1])
    return jnp.where(valid[:, :, None], taken, jnp.zeros_like(taken))


def compact_rows(slots, loads_in, count):
    sources, depth = (slots.shape[0], slots.shape[1])
    offsets = jnp.cumsum(loads_in) - loads_in
    ends = offsets + loads_in
    place = jnp.arange(count, dtype=jnp.int32)
    owner = jnp.sum((ends[:, None] <= place[None, :]).astype(jnp.int32), axis=0)
    owner = jnp.minimum(owner, sources - 1)
    inner = place - jnp.take(offsets, owner)
    valid = place < jnp.sum(loads_in)
    flat = jnp.where(valid, owner * depth + inner, 0)
    taken = jnp.take(slots.reshape(sources * depth, slots.shape[2]), flat, axis=0)
    return jnp.where(valid[:, None], taken, jnp.zeros_like(taken))


def deal_out(rows, loads_out, firsts_out, loads_in, count):
    slots = pack_slots(rows, loads_out, firsts_out, MOST)
    arrived = lax.all_to_all(slots, "fsdp", split_axis=0, concat_axis=0, tiled=True)
    return compact_rows(arrived, loads_in, count)


def per_device(x_src, doc_lengths, doc_dests, w_gate, w_up, w_down, basis, out_cotangent):
    hidden_width = w_gate.shape[1]
    tok = x_src.shape[0]
    recv = out_cotangent.shape[0]
    loads, firsts = deal_tables(doc_lengths, doc_dests)
    myself = lax.axis_index("fsdp")
    loads_out = jnp.take(loads, myself, axis=0)
    firsts_out = jnp.take(firsts, myself, axis=0)
    loads_in = jnp.take(loads, myself, axis=1)
    rows_of = token_rows(doc_lengths, doc_dests, loads, tok, recv)
    contract_rows = (((0,), (0,)), ((), ()))
    contract_cols = (((1,), (1,)), ((), ()))

    xall = lax.all_gather(x_src, "fsdp", axis=0, tiled=True)
    dy_dealt = lax.all_gather(out_cotangent, "fsdp", axis=0, tiled=True)
    dyall = jnp.take(dy_dealt, rows_of, axis=0)

    first = settle(jnp.dot(xall, w_gate, preferred_element_type=jnp.float32))
    second = settle(jnp.dot(xall, w_up, preferred_element_type=jnp.float32))
    both = lax.psum(
        jnp.concatenate([first, second], axis=1).astype(jnp.bfloat16), "dp"
    ).astype(jnp.float32)
    gate = both[:, :hidden_width]
    up = both[:, hidden_width:]
    sig = jax.nn.sigmoid(gate)
    hidden = (gate * sig * up).astype(jnp.bfloat16)
    out_part = settle(jnp.dot(hidden, w_down, preferred_element_type=jnp.float32))
    out_src = lax.psum_scatter(
        out_part.astype(jnp.bfloat16), "fsdp", scatter_dimension=0, tiled=True
    )
    layer_out = deal_out(out_src, loads_out, firsts_out, loads_in, recv)

    hg_part = settle(
        lax.dot_general(dyall, w_down, contract_cols, preferred_element_type=jnp.float32)
    )
    hidden_grad = lax.psum(hg_part.astype(jnp.bfloat16), "dp").astype(jnp.float32)
    gate_grad = (hidden_grad * up * sig * (1.0 + gate * (1.0 - sig))).astype(jnp.bfloat16)
    up_grad = (hidden_grad * gate * sig).astype(jnp.bfloat16)
    grad_down = lax.dot_general(hidden, dyall, contract_rows, preferred_element_type=jnp.float32)
    raw_gate = lax.dot_general(xall, gate_grad, contract_rows, preferred_element_type=jnp.float32)
    raw_up = lax.dot_general(xall, up_grad, contract_rows, preferred_element_type=jnp.float32)
    total = lax.dot_general(
        gate_grad, w_gate, contract_cols, preferred_element_type=jnp.float32
    )
    total = total + lax.dot_general(
        up_grad, w_up, contract_cols, preferred_element_type=jnp.float32
    )
    in_src = lax.psum_scatter(
        settle(total).astype(jnp.bfloat16), "fsdp", scatter_dimension=0, tiled=True
    )
    input_grad = deal_out(in_src, loads_out, firsts_out, loads_in, recv)

    keys_local = jnp.dot(xall, basis, preferred_element_type=jnp.float32)
    keys_all = lax.psum(keys_local.astype(jnp.bfloat16), "dp")
    over_gate = lax.dot_general(keys_all, gate_grad, contract_rows, preferred_element_type=jnp.float32)
    over_up = lax.dot_general(keys_all, up_grad, contract_rows, preferred_element_type=jnp.float32)
    grad_gate = raw_gate - jnp.dot(basis, over_gate, preferred_element_type=jnp.float32)
    grad_up = raw_up - jnp.dot(basis, over_up, preferred_element_type=jnp.float32)
    return (layer_out, input_grad, grad_gate, grad_up, grad_down)


def solution(mesh):
    return jax.shard_map(
        per_device,
        mesh=mesh,
        in_specs=(
            P("fsdp", "dp"),
            P(),
            P(),
            P("dp", "fsdp"),
            P("dp", "fsdp"),
            P("fsdp", "dp"),
            P("dp", None),
            P("fsdp", "dp"),
        ),
        out_specs=(
            P("fsdp", "dp"),
            P("fsdp", "dp"),
            P("dp", "fsdp"),
            P("dp", "fsdp"),
            P("fsdp", "dp"),
        ),
        check_vma=False,
    )
```

```python
import functools

import jax
import jax.numpy as jnp
from jax import lax
from jax.sharding import PartitionSpec as P

MOST = 16


def deal_tables(doc_lengths, doc_dests):
    groups = doc_lengths.shape[0]
    starts = jnp.cumsum(doc_lengths, axis=1) - doc_lengths
    targets = jnp.arange(groups, dtype=jnp.int32)
    hits = (doc_dests[:, :, None] == targets[None, None, :]).astype(jnp.int32)
    loads = jnp.sum(doc_lengths[:, :, None] * hits, axis=1)
    firsts = jnp.sum(starts[:, :, None] * hits, axis=1)
    return (loads, firsts)


def token_rows(doc_lengths, doc_dests, loads, tok, recv):
    starts = jnp.cumsum(doc_lengths, axis=1) - doc_lengths
    ends = starts + doc_lengths
    offsets = jnp.cumsum(loads, axis=0) - loads
    t = jnp.arange(tok, dtype=jnp.int32)
    doc_of = jnp.sum((ends[:, :, None] <= t[None, None, :]).astype(jnp.int32), axis=1)
    doc_of = jnp.minimum(doc_of, doc_lengths.shape[1] - 1)
    dst = jnp.take_along_axis(doc_dests, doc_of, axis=1)
    st = jnp.take_along_axis(starts, doc_of, axis=1)
    off = jnp.take_along_axis(offsets, dst, axis=1)
    row = dst * recv + off + t[None, :] - st
    return jnp.clip(row, 0, loads.shape[0] * recv - 1).reshape(-1)


def settle(term):
    return lax.optimization_barrier(term.astype(jnp.bfloat16)).astype(jnp.float32)


def deal_index(doc_lengths, doc_dests, loads, firsts, tok, recv):
    sources = loads.shape[0]
    offsets = jnp.cumsum(loads, axis=0) - loads
    ends = offsets + loads
    place = jnp.arange(recv, dtype=jnp.int32)
    owner = jnp.sum((ends[:, :, None] <= place[None, None, :]).astype(jnp.int32), axis=0)
    owner = jnp.minimum(owner, sources - 1)
    pick = (owner[None, :, :] == jnp.arange(sources, dtype=jnp.int32)[:, None, None]).astype(jnp.int32)
    own_offset = jnp.sum(pick * offsets[:, :, None], axis=0)
    own_first = jnp.sum(pick * firsts[:, :, None], axis=0)
    valid = place[None, :] < jnp.sum(loads, axis=0)[:, None]
    index = owner * tok + own_first + place[None, :] - own_offset
    index = jnp.where(valid, index, 0)
    return jnp.clip(index, 0, sources * tok - 1).reshape(-1), valid


def reduce_rows(part, axis, n):
    rows, cols = part.shape
    got = lax.all_to_all(part.astype(jnp.bfloat16).reshape(n, rows // n, cols), axis, 0, 0, tiled=True)
    return jnp.sum(got.astype(jnp.float32), axis=0)


def gather_rows(block, axis, n):
    rows, cols = block.shape
    got = lax.all_to_all(jnp.broadcast_to(block[None], (n, rows, cols)), axis, 0, 0, tiled=True)
    return got.reshape(n * rows, cols)


def reduce_dealt(part, index, valid, n):
    cols = part.shape[1]
    send = jnp.take(part.astype(jnp.bfloat16), index, axis=0).reshape(valid.shape[0], valid.shape[1], cols)
    send = jnp.where(valid[:, :, None], send, jnp.zeros_like(send))
    got = lax.all_to_all(send, "fsdp", 0, 0, tiled=True)
    return jnp.sum(got.astype(jnp.float32), axis=0).astype(jnp.bfloat16)


def per_device(n_dp, n_fsdp, x_src, doc_lengths, doc_dests, w_gate, w_up, w_down, basis, out_cotangent):
    hidden_width = w_gate.shape[1]
    tok = x_src.shape[0]
    recv = out_cotangent.shape[0]
    loads, firsts = deal_tables(doc_lengths, doc_dests)
    rows_of = token_rows(doc_lengths, doc_dests, loads, tok, recv)
    index, valid = deal_index(doc_lengths, doc_dests, loads, firsts, tok, recv)
    contract_rows = (((0,), (0,)), ((), ()))
    contract_cols = (((1,), (1,)), ((), ()))

    xall = gather_rows(x_src, "fsdp", n_fsdp)
    dy_dealt = lax.all_gather(out_cotangent, "fsdp", axis=0, tiled=True)
    dyall = jnp.take(dy_dealt, rows_of, axis=0)
    first = jnp.dot(xall, w_gate, preferred_element_type=jnp.float32)
    second = jnp.dot(xall, w_up, preferred_element_type=jnp.float32)
    keys_local = jnp.dot(xall, basis, preferred_element_type=jnp.float32)
    both = reduce_rows(jnp.concatenate([first, second, keys_local], axis=1), "dp", n_dp)
    gate = both[:, :hidden_width]
    up = both[:, hidden_width:2 * hidden_width]
    keys = both[:, 2 * hidden_width:].astype(jnp.bfloat16)
    sig = jax.nn.sigmoid(gate)
    hidden = (gate * sig * up).astype(jnp.bfloat16)
    gathered = gather_rows(jnp.concatenate([hidden, keys], axis=1), "dp", n_dp)
    hall = gathered[:, :hidden_width]
    keys_all = gathered[:, hidden_width:]
    out_part = jnp.dot(hall, w_down, preferred_element_type=jnp.float32)
    layer_out = reduce_dealt(out_part, index, valid, n_fsdp)

    hg_part = lax.dot_general(dyall, w_down, contract_cols, preferred_element_type=jnp.float32)
    hidden_grad = reduce_rows(hg_part, "dp", n_dp)
    gate_grad = (hidden_grad * up * sig * (1.0 + gate * (1.0 - sig))).astype(jnp.bfloat16)
    up_grad = (hidden_grad * gate * sig).astype(jnp.bfloat16)
    grads = gather_rows(jnp.concatenate([gate_grad, up_grad], axis=1), "dp", n_dp)
    gate_all = grads[:, :hidden_width]
    up_all = grads[:, hidden_width:]
    grad_down = lax.dot_general(hall, dyall, contract_rows, preferred_element_type=jnp.float32)
    raw_gate = lax.dot_general(xall, gate_all, contract_rows, preferred_element_type=jnp.float32)
    raw_up = lax.dot_general(xall, up_all, contract_rows, preferred_element_type=jnp.float32)
    total = lax.dot_general(gate_all, w_gate, contract_cols, preferred_element_type=jnp.float32)
    total = total + lax.dot_general(up_all, w_up, contract_cols, preferred_element_type=jnp.float32)
    input_grad = reduce_dealt(total, index, valid, n_fsdp)

    over_gate = lax.dot_general(keys_all, gate_all, contract_rows, preferred_element_type=jnp.float32)
    over_up = lax.dot_general(keys_all, up_all, contract_rows, preferred_element_type=jnp.float32)
    grad_gate = raw_gate - jnp.dot(basis, over_gate, preferred_element_type=jnp.float32)
    grad_up = raw_up - jnp.dot(basis, over_up, preferred_element_type=jnp.float32)
    return (layer_out, input_grad, grad_gate, grad_up, grad_down)


def solution(mesh):
    body = functools.partial(per_device, mesh.shape["dp"], mesh.shape["fsdp"])
    return jax.shard_map(
        body,
        mesh=mesh,
        in_specs=(
            P("fsdp", "dp"),
            P(),
            P(),
            P("dp", "fsdp"),
            P("dp", "fsdp"),
            P("fsdp", "dp"),
            P("dp", None),
            P("fsdp", "dp"),
        ),
        out_specs=(
            P("fsdp", "dp"),
            P("fsdp", "dp"),
            P("dp", "fsdp"),
            P("dp", "fsdp"),
            P("fsdp", "dp"),
        ),
        check_vma=False,
    )
```

```python
import functools

import jax
import jax.numpy as jnp
from jax import lax
from jax.sharding import PartitionSpec as P

MOST = 16


def deal_tables(doc_lengths, doc_dests):
    groups = doc_lengths.shape[0]
    starts = jnp.cumsum(doc_lengths, axis=1) - doc_lengths
    targets = jnp.arange(groups, dtype=jnp.int32)
    hits = (doc_dests[:, :, None] == targets[None, None, :]).astype(jnp.int32)
    loads = jnp.sum(doc_lengths[:, :, None] * hits, axis=1)
    firsts = jnp.sum(starts[:, :, None] * hits, axis=1)
    return (loads, firsts)


def token_rows(doc_lengths, doc_dests, loads, tok, recv):
    sources, ndoc = doc_lengths.shape
    starts = jnp.cumsum(doc_lengths, axis=1) - doc_lengths
    ends = starts + doc_lengths
    offsets = jnp.cumsum(loads, axis=0) - loads
    t = jnp.arange(tok, dtype=jnp.int32)
    doc_of = jnp.sum((ends[:, :, None] <= t[None, None, :]).astype(jnp.int32), axis=1)
    doc_of = jnp.minimum(doc_of, ndoc - 1)
    hit = (doc_of[:, :, None] == jnp.arange(ndoc, dtype=jnp.int32)[None, None, :]).astype(jnp.int32)
    dst = jnp.sum(hit * doc_dests[:, None, :], axis=2)
    st = jnp.sum(hit * starts[:, None, :], axis=2)
    to = (dst[:, :, None] == jnp.arange(sources, dtype=jnp.int32)[None, None, :]).astype(jnp.int32)
    off = jnp.sum(to * offsets[:, None, :], axis=2)
    row = dst * recv + off + t[None, :] - st
    return row.reshape(-1)


def settle(term):
    return lax.optimization_barrier(term.astype(jnp.bfloat16)).astype(jnp.float32)


def reduce_rows(part, axis, n):
    rows, cols = part.shape
    got = lax.all_to_all(part.astype(jnp.bfloat16).reshape(n, rows // n, cols), axis, 0, 0, tiled=True)
    return jnp.sum(got.astype(jnp.float32), axis=0)


def gather_rows(block, axis, n):
    rows, cols = block.shape
    got = lax.all_to_all(jnp.broadcast_to(block[None], (n, rows, cols)), axis, 0, 0, tiled=True)
    return got.reshape(n * rows, cols)


def reduce_dealt(part, pick, blocks):
    cols = part.shape[1]
    contract_rows = (((0,), (0,)), ((), ()))
    send = lax.dot_general(pick, part.astype(jnp.bfloat16), contract_rows, preferred_element_type=jnp.float32)
    send = send.astype(jnp.bfloat16).reshape(blocks, -1, cols)
    got = lax.all_to_all(send, "fsdp", 0, 0, tiled=True)
    return jnp.sum(got.astype(jnp.float32), axis=0).astype(jnp.bfloat16)


def per_device(n_dp, n_fsdp, x_src, doc_lengths, doc_dests, w_gate, w_up, w_down, basis, out_cotangent):
    hidden_width = w_gate.shape[1]
    tok = x_src.shape[0]
    recv = out_cotangent.shape[0]
    loads, firsts = deal_tables(doc_lengths, doc_dests)
    rows_of = token_rows(doc_lengths, doc_dests, loads, tok, recv)
    dealt_rows = jnp.arange(n_fsdp * recv, dtype=jnp.int32)
    pick = (rows_of[:, None] == dealt_rows[None, :]).astype(jnp.bfloat16)
    contract_rows = (((0,), (0,)), ((), ()))
    contract_cols = (((1,), (1,)), ((), ()))

    xall = gather_rows(x_src, "fsdp", n_fsdp)
    dy_dealt = lax.all_gather(out_cotangent, "fsdp", axis=0, tiled=True)
    dyall = jnp.dot(pick, dy_dealt, preferred_element_type=jnp.float32).astype(jnp.bfloat16)
    first = jnp.dot(xall, w_gate, preferred_element_type=jnp.float32)
    second = jnp.dot(xall, w_up, preferred_element_type=jnp.float32)
    keys_local = jnp.dot(xall, basis, preferred_element_type=jnp.float32)
    both = reduce_rows(jnp.concatenate([first, second, keys_local], axis=1), "dp", n_dp)
    gate = both[:, :hidden_width]
    up = both[:, hidden_width:2 * hidden_width]
    keys = both[:, 2 * hidden_width:].astype(jnp.bfloat16)
    sig = jax.nn.sigmoid(gate)
    hidden = (gate * sig * up).astype(jnp.bfloat16)
    gathered = gather_rows(jnp.concatenate([hidden, keys], axis=1), "dp", n_dp)
    hall = gathered[:, :hidden_width]
    keys_all = gathered[:, hidden_width:]
    out_part = jnp.dot(hall, w_down, preferred_element_type=jnp.float32)
    layer_out = reduce_dealt(out_part, pick, n_fsdp)

    hg_part = lax.dot_general(dyall, w_down, contract_cols, preferred_element_type=jnp.float32)
    hidden_grad = reduce_rows(hg_part, "dp", n_dp)
    gate_grad = (hidden_grad * up * sig * (1.0 + gate * (1.0 - sig))).astype(jnp.bfloat16)
    up_grad = (hidden_grad * gate * sig).astype(jnp.bfloat16)
    grads = gather_rows(jnp.concatenate([gate_grad, up_grad], axis=1), "dp", n_dp)
    gate_all = grads[:, :hidden_width]
    up_all = grads[:, hidden_width:]
    grad_down = lax.dot_general(hall, dyall, contract_rows, preferred_element_type=jnp.float32)
    total = lax.dot_general(gate_all, w_gate, contract_cols, preferred_element_type=jnp.float32)
    total = total + lax.dot_general(up_all, w_up, contract_cols, preferred_element_type=jnp.float32)
    input_grad = reduce_dealt(total, pick, n_fsdp)

    x_t = xall.T.astype(jnp.float32)
    keys_t = lax.dot_general(basis, keys_all, contract_cols, preferred_element_type=jnp.float32)
    xp_t = (x_t - keys_t).astype(jnp.bfloat16)
    grad_gate = jnp.dot(xp_t, gate_all, preferred_element_type=jnp.float32)
    grad_up = jnp.dot(xp_t, up_all, preferred_element_type=jnp.float32)
    return (layer_out, input_grad, grad_gate, grad_up, grad_down)


def solution(mesh):
    body = functools.partial(per_device, mesh.shape["dp"], mesh.shape["fsdp"])
    return jax.shard_map(
        body,
        mesh=mesh,
        in_specs=(
            P("fsdp", "dp"),
            P(),
            P(),
            P("dp", "fsdp"),
            P("dp", "fsdp"),
            P("fsdp", "dp"),
            P("dp", None),
            P("fsdp", "dp"),
        ),
        out_specs=(
            P("fsdp", "dp"),
            P("fsdp", "dp"),
            P("dp", "fsdp"),
            P("dp", "fsdp"),
            P("fsdp", "dp"),
        ),
        check_vma=False,
    )
```

```python
import functools

import jax
import jax.numpy as jnp
from jax import lax
from jax.sharding import PartitionSpec as P

MOST = 16


def deal_tables(doc_lengths, doc_dests):
    groups = doc_lengths.shape[0]
    starts = jnp.cumsum(doc_lengths, axis=1) - doc_lengths
    targets = jnp.arange(groups, dtype=jnp.int32)
    hits = (doc_dests[:, :, None] == targets[None, None, :]).astype(jnp.int32)
    loads = jnp.sum(doc_lengths[:, :, None] * hits, axis=1)
    firsts = jnp.sum(starts[:, :, None] * hits, axis=1)
    return (loads, firsts)


def token_rows(doc_lengths, doc_dests, loads, tok, recv):
    sources, ndoc = doc_lengths.shape
    starts = jnp.cumsum(doc_lengths, axis=1) - doc_lengths
    ends = starts + doc_lengths
    offsets = jnp.cumsum(loads, axis=0) - loads
    t = jnp.arange(tok, dtype=jnp.int32)
    doc_of = jnp.sum((ends[:, :, None] <= t[None, None, :]).astype(jnp.int32), axis=1)
    doc_of = jnp.minimum(doc_of, ndoc - 1)
    hit = (doc_of[:, :, None] == jnp.arange(ndoc, dtype=jnp.int32)[None, None, :]).astype(jnp.int32)
    dst = jnp.sum(hit * doc_dests[:, None, :], axis=2)
    st = jnp.sum(hit * starts[:, None, :], axis=2)
    to = (dst[:, :, None] == jnp.arange(sources, dtype=jnp.int32)[None, None, :]).astype(jnp.int32)
    off = jnp.sum(to * offsets[:, None, :], axis=2)
    row = dst * recv + off + t[None, :] - st
    return row.reshape(-1)


def settle(term):
    return lax.optimization_barrier(term.astype(jnp.bfloat16)).astype(jnp.float32)


def reduce_rows(part, axis, n):
    rows, cols = part.shape
    got = lax.all_to_all(part.astype(jnp.bfloat16).reshape(n, rows // n, cols), axis, 0, 0, tiled=True)
    return jnp.sum(got.astype(jnp.float32), axis=0)


def gather_rows(block, axis, n):
    rows, cols = block.shape
    got = lax.all_to_all(jnp.broadcast_to(block[None], (n, rows, cols)), axis, 0, 0, tiled=True)
    return got.reshape(n * rows, cols)


def reduce_dealt(part, pick, blocks):
    cols = part.shape[1]
    contract_rows = (((0,), (0,)), ((), ()))
    send = lax.dot_general(pick, part.astype(jnp.bfloat16), contract_rows, preferred_element_type=jnp.float32)
    send = send.astype(jnp.bfloat16).reshape(blocks, -1, cols)
    got = lax.all_to_all(send, "fsdp", 0, 0, tiled=True)
    return jnp.sum(got.astype(jnp.float32), axis=0).astype(jnp.bfloat16)


def per_device(n_dp, n_fsdp, x_src, doc_lengths, doc_dests, w_gate, w_up, w_down, basis, out_cotangent):
    hidden_width = w_gate.shape[1]
    tok = x_src.shape[0]
    recv = out_cotangent.shape[0]
    loads, firsts = deal_tables(doc_lengths, doc_dests)
    rows_of = token_rows(doc_lengths, doc_dests, loads, tok, recv)
    dealt_rows = jnp.arange(n_fsdp * recv, dtype=jnp.int32)
    pick = (rows_of[:, None] == dealt_rows[None, :]).astype(jnp.bfloat16)
    contract_rows = (((0,), (0,)), ((), ()))
    contract_cols = (((1,), (1,)), ((), ()))

    xall = gather_rows(x_src, "fsdp", n_fsdp)
    dy_dealt = lax.all_gather(out_cotangent, "fsdp", axis=0, tiled=True)
    dyall = jnp.dot(pick, dy_dealt, preferred_element_type=jnp.float32).astype(jnp.bfloat16)
    first = jnp.dot(xall, w_gate, preferred_element_type=jnp.float32)
    second = jnp.dot(xall, w_up, preferred_element_type=jnp.float32)
    keys_local = jnp.dot(xall, basis, preferred_element_type=jnp.float32)
    both = reduce_rows(jnp.concatenate([first, second, keys_local], axis=1), "dp", n_dp)
    gate = both[:, :hidden_width]
    up = both[:, hidden_width:2 * hidden_width]
    keys = both[:, 2 * hidden_width:].astype(jnp.bfloat16)
    sig = jax.nn.sigmoid(gate)
    hidden = (gate * sig * up).astype(jnp.bfloat16)
    gathered = gather_rows(jnp.concatenate([hidden, keys], axis=1), "dp", n_dp)
    hall = gathered[:, :hidden_width]
    keys_all = gathered[:, hidden_width:]
    out_part = jnp.dot(hall, w_down, preferred_element_type=jnp.float32)
    layer_out = reduce_dealt(out_part, pick, n_fsdp)

    hg_part = lax.dot_general(dyall, w_down, contract_cols, preferred_element_type=jnp.float32)
    hidden_grad = reduce_rows(hg_part, "dp", n_dp)
    gate_grad = (hidden_grad * up * sig * (1.0 + gate * (1.0 - sig))).astype(jnp.bfloat16)
    up_grad = (hidden_grad * gate * sig).astype(jnp.bfloat16)
    grads = lax.all_gather(jnp.concatenate([gate_grad, up_grad], axis=1), "dp", axis=0, tiled=True)
    gate_all = grads[:, :hidden_width]
    up_all = grads[:, hidden_width:]
    grad_down = lax.dot_general(hall, dyall, contract_rows, preferred_element_type=jnp.float32)
    total = lax.dot_general(gate_all, w_gate, contract_cols, preferred_element_type=jnp.float32)
    total = total + lax.dot_general(up_all, w_up, contract_cols, preferred_element_type=jnp.float32)
    input_grad = reduce_dealt(total, pick, n_fsdp)

    x_t = xall.T.astype(jnp.float32)
    keys_t = lax.dot_general(basis, keys_all, contract_cols, preferred_element_type=jnp.float32)
    xp_t = (x_t - keys_t).astype(jnp.bfloat16)
    grad_gate = jnp.dot(xp_t, gate_all, preferred_element_type=jnp.float32)
    grad_up = jnp.dot(xp_t, up_all, preferred_element_type=jnp.float32)
    return (layer_out, input_grad, grad_gate, grad_up, grad_down)


def solution(mesh):
    body = functools.partial(per_device, mesh.shape["dp"], mesh.shape["fsdp"])
    return jax.shard_map(
        body,
        mesh=mesh,
        in_specs=(
            P("fsdp", "dp"),
            P(),
            P(),
            P("dp", "fsdp"),
            P("dp", "fsdp"),
            P("fsdp", "dp"),
            P("dp", None),
            P("fsdp", "dp"),
        ),
        out_specs=(
            P("fsdp", "dp"),
            P("fsdp", "dp"),
            P("dp", "fsdp"),
            P("dp", "fsdp"),
            P("fsdp", "dp"),
        ),
        check_vma=False,
    )
```

```python
import functools

import jax
import jax.numpy as jnp
from jax import lax
from jax.sharding import PartitionSpec as P

MOST = 16


def deal_tables(doc_lengths, doc_dests):
    groups = doc_lengths.shape[0]
    starts = jnp.cumsum(doc_lengths, axis=1) - doc_lengths
    targets = jnp.arange(groups, dtype=jnp.int32)
    hits = (doc_dests[:, :, None] == targets[None, None, :]).astype(jnp.int32)
    loads = jnp.sum(doc_lengths[:, :, None] * hits, axis=1)
    firsts = jnp.sum(starts[:, :, None] * hits, axis=1)
    return (loads, firsts)


def token_rows(doc_lengths, doc_dests, loads, tok, recv):
    sources, ndoc = doc_lengths.shape
    starts = jnp.cumsum(doc_lengths, axis=1) - doc_lengths
    ends = starts + doc_lengths
    offsets = jnp.cumsum(loads, axis=0) - loads
    t = jnp.arange(tok, dtype=jnp.int32)
    doc_of = jnp.sum((ends[:, :, None] <= t[None, None, :]).astype(jnp.int32), axis=1)
    doc_of = jnp.minimum(doc_of, ndoc - 1)
    hit = (doc_of[:, :, None] == jnp.arange(ndoc, dtype=jnp.int32)[None, None, :]).astype(jnp.int32)
    dst = jnp.sum(hit * doc_dests[:, None, :], axis=2)
    st = jnp.sum(hit * starts[:, None, :], axis=2)
    to = (dst[:, :, None] == jnp.arange(sources, dtype=jnp.int32)[None, None, :]).astype(jnp.int32)
    off = jnp.sum(to * offsets[:, None, :], axis=2)
    row = dst * recv + off + t[None, :] - st
    return row.reshape(-1)


def settle(term):
    return lax.optimization_barrier(term.astype(jnp.bfloat16)).astype(jnp.float32)


def reduce_rows(part, axis, n):
    rows, cols = part.shape
    got = lax.all_to_all(part.astype(jnp.bfloat16).reshape(n, rows // n, cols), axis, 0, 0, tiled=True)
    return jnp.sum(got.astype(jnp.float32), axis=0)


def gather_rows(block, axis, n):
    rows, cols = block.shape
    got = lax.all_to_all(jnp.broadcast_to(block[None], (n, rows, cols)), axis, 0, 0, tiled=True)
    return got.reshape(n * rows, cols)


def reduce_dealt(part, pick, blocks):
    cols = part.shape[1]
    contract_rows = (((0,), (0,)), ((), ()))
    send = lax.dot_general(pick, part.astype(jnp.bfloat16), contract_rows, preferred_element_type=jnp.float32)
    send = send.astype(jnp.bfloat16).reshape(blocks, -1, cols)
    got = lax.all_to_all(send, "fsdp", 0, 0, tiled=True)
    return jnp.sum(got.astype(jnp.float32), axis=0).astype(jnp.bfloat16)


def per_device(n_dp, n_fsdp, x_src, doc_lengths, doc_dests, w_gate, w_up, w_down, basis, out_cotangent):
    hidden_width = w_gate.shape[1]
    tok = x_src.shape[0]
    recv = out_cotangent.shape[0]
    loads, firsts = deal_tables(doc_lengths, doc_dests)
    rows_of = token_rows(doc_lengths, doc_dests, loads, tok, recv)
    dealt_rows = jnp.arange(n_fsdp * recv, dtype=jnp.int32)
    pick = (rows_of[:, None] == dealt_rows[None, :]).astype(jnp.bfloat16)
    contract_rows = (((0,), (0,)), ((), ()))
    contract_cols = (((1,), (1,)), ((), ()))

    xall = gather_rows(x_src, "fsdp", n_fsdp)
    dy_dealt = lax.all_gather(out_cotangent, "fsdp", axis=0, tiled=True)
    dyall = jnp.dot(pick, dy_dealt, preferred_element_type=jnp.float32).astype(jnp.bfloat16)
    keys_part = jnp.dot(x_src, basis, preferred_element_type=jnp.float32).astype(jnp.bfloat16)
    keys_dp = lax.all_gather(keys_part, "dp", axis=0, tiled=False)
    keys_src = jnp.sum(keys_dp.astype(jnp.float32), axis=0).astype(jnp.bfloat16)
    keys_all = lax.all_gather(keys_src, "fsdp", axis=0, tiled=True)

    first = jnp.dot(xall, w_gate, preferred_element_type=jnp.float32)
    second = jnp.dot(xall, w_up, preferred_element_type=jnp.float32)
    both = reduce_rows(jnp.concatenate([first, second], axis=1), "dp", n_dp)
    gate = both[:, :hidden_width]
    up = both[:, hidden_width:]
    sig = jax.nn.sigmoid(gate)
    hidden = (gate * sig * up).astype(jnp.bfloat16)
    hall = gather_rows(hidden, "dp", n_dp)
    out_part = jnp.dot(hall, w_down, preferred_element_type=jnp.float32)
    layer_out = reduce_dealt(out_part, pick, n_fsdp)

    hg_part = lax.dot_general(dyall, w_down, contract_cols, preferred_element_type=jnp.float32)
    hidden_grad = reduce_rows(hg_part, "dp", n_dp)
    gate_grad = (hidden_grad * up * sig * (1.0 + gate * (1.0 - sig))).astype(jnp.bfloat16)
    up_grad = (hidden_grad * gate * sig).astype(jnp.bfloat16)
    grads = gather_rows(jnp.concatenate([gate_grad, up_grad], axis=1), "dp", n_dp)
    gate_all = grads[:, :hidden_width]
    up_all = grads[:, hidden_width:]
    grad_down = lax.dot_general(hall, dyall, contract_rows, preferred_element_type=jnp.float32)
    total = lax.dot_general(gate_all, w_gate, contract_cols, preferred_element_type=jnp.float32)
    total = total + lax.dot_general(up_all, w_up, contract_cols, preferred_element_type=jnp.float32)
    input_grad = reduce_dealt(total, pick, n_fsdp)

    x_t = xall.T.astype(jnp.float32)
    keys_t = lax.dot_general(basis, keys_all, contract_cols, preferred_element_type=jnp.float32)
    xp_t = (x_t - keys_t).astype(jnp.bfloat16)
    grad_gate = jnp.dot(xp_t, gate_all, preferred_element_type=jnp.float32)
    grad_up = jnp.dot(xp_t, up_all, preferred_element_type=jnp.float32)
    return (layer_out, input_grad, grad_gate, grad_up, grad_down)


def solution(mesh):
    body = functools.partial(per_device, mesh.shape["dp"], mesh.shape["fsdp"])
    return jax.shard_map(
        body,
        mesh=mesh,
        in_specs=(
            P("fsdp", "dp"),
            P(),
            P(),
            P("dp", "fsdp"),
            P("dp", "fsdp"),
            P("fsdp", "dp"),
            P("dp", None),
            P("fsdp", "dp"),
        ),
        out_specs=(
            P("fsdp", "dp"),
            P("fsdp", "dp"),
            P("dp", "fsdp"),
            P("dp", "fsdp"),
            P("fsdp", "dp"),
        ),
        check_vma=False,
    )
```

```python
import functools

import jax
import jax.numpy as jnp
from jax import lax
from jax.sharding import PartitionSpec as P

MOST = 16


def deal_tables(doc_lengths, doc_dests):
    groups = doc_lengths.shape[0]
    starts = jnp.cumsum(doc_lengths, axis=1) - doc_lengths
    targets = jnp.arange(groups, dtype=jnp.int32)
    hits = (doc_dests[:, :, None] == targets[None, None, :]).astype(jnp.int32)
    loads = jnp.sum(doc_lengths[:, :, None] * hits, axis=1)
    firsts = jnp.sum(starts[:, :, None] * hits, axis=1)
    return (loads, firsts)


def token_rows(doc_lengths, doc_dests, loads, tok, recv):
    sources, ndoc = doc_lengths.shape
    starts = jnp.cumsum(doc_lengths, axis=1) - doc_lengths
    ends = starts + doc_lengths
    offsets = jnp.cumsum(loads, axis=0) - loads
    t = jnp.arange(tok, dtype=jnp.int32)
    doc_of = jnp.sum((ends[:, :, None] <= t[None, None, :]).astype(jnp.int32), axis=1)
    doc_of = jnp.minimum(doc_of, ndoc - 1)
    hit = (doc_of[:, :, None] == jnp.arange(ndoc, dtype=jnp.int32)[None, None, :]).astype(jnp.int32)
    dst = jnp.sum(hit * doc_dests[:, None, :], axis=2)
    st = jnp.sum(hit * starts[:, None, :], axis=2)
    to = (dst[:, :, None] == jnp.arange(sources, dtype=jnp.int32)[None, None, :]).astype(jnp.int32)
    off = jnp.sum(to * offsets[:, None, :], axis=2)
    row = dst * recv + off + t[None, :] - st
    return row.reshape(-1)


def settle(term):
    return lax.optimization_barrier(term.astype(jnp.bfloat16)).astype(jnp.float32)


def reduce_rows(part, axis, n):
    rows, cols = part.shape
    got = lax.all_to_all(part.astype(jnp.bfloat16).reshape(n, rows // n, cols), axis, 0, 0, tiled=True)
    return jnp.sum(got.astype(jnp.float32), axis=0)


def gather_rows(block, axis, n):
    rows, cols = block.shape
    got = lax.all_to_all(jnp.broadcast_to(block[None], (n, rows, cols)), axis, 0, 0, tiled=True)
    return got.reshape(n * rows, cols)


def reduce_dealt(part, pick, blocks):
    cols = part.shape[1]
    contract_rows = (((0,), (0,)), ((), ()))
    send = lax.dot_general(pick, part.astype(jnp.bfloat16), contract_rows, preferred_element_type=jnp.float32)
    send = send.astype(jnp.bfloat16).reshape(blocks, -1, cols)
    got = lax.all_to_all(send, "fsdp", 0, 0, tiled=True)
    return jnp.sum(got.astype(jnp.float32), axis=0).astype(jnp.bfloat16)


def per_device(n_dp, n_fsdp, x_src, doc_lengths, doc_dests, w_gate, w_up, w_down, basis, out_cotangent):
    hidden_width = w_gate.shape[1]
    tok = x_src.shape[0]
    recv = out_cotangent.shape[0]
    loads, firsts = deal_tables(doc_lengths, doc_dests)
    rows_of = token_rows(doc_lengths, doc_dests, loads, tok, recv)
    dealt_rows = jnp.arange(n_fsdp * recv, dtype=jnp.int32)
    pick = (rows_of[:, None] == dealt_rows[None, :]).astype(jnp.bfloat16)
    contract_rows = (((0,), (0,)), ((), ()))
    contract_cols = (((1,), (1,)), ((), ()))

    xall = gather_rows(x_src, "fsdp", n_fsdp)
    dy_dealt = lax.all_gather(out_cotangent, "fsdp", axis=0, tiled=True)
    dyall = jnp.dot(pick, dy_dealt, preferred_element_type=jnp.float32).astype(jnp.bfloat16)
    first = jnp.dot(xall, w_gate, preferred_element_type=jnp.float32)
    second = jnp.dot(xall, w_up, preferred_element_type=jnp.float32)
    keys_local = jnp.dot(xall, basis, preferred_element_type=jnp.float32)
    both = reduce_rows(jnp.concatenate([first, second, keys_local], axis=1), "dp", n_dp)
    gate = both[:, :hidden_width]
    up = both[:, hidden_width:2 * hidden_width]
    keys = both[:, 2 * hidden_width:].astype(jnp.bfloat16)
    sig = jax.nn.sigmoid(gate)
    hidden = (gate * sig * up).astype(jnp.bfloat16)

    hg_part = lax.dot_general(dyall, w_down, contract_cols, preferred_element_type=jnp.float32)
    hidden_grad = reduce_rows(hg_part, "dp", n_dp)
    gate_grad = (hidden_grad * up * sig * (1.0 + gate * (1.0 - sig))).astype(jnp.bfloat16)
    up_grad = (hidden_grad * gate * sig).astype(jnp.bfloat16)
    gathered = gather_rows(jnp.concatenate([hidden, gate_grad, up_grad, keys], axis=1), "dp", n_dp)
    hall = gathered[:, :hidden_width]
    gate_all = gathered[:, hidden_width:2 * hidden_width]
    up_all = gathered[:, 2 * hidden_width:3 * hidden_width]
    keys_all = gathered[:, 3 * hidden_width:]
    out_part = jnp.dot(hall, w_down, preferred_element_type=jnp.float32)
    grad_down = lax.dot_general(hall, dyall, contract_rows, preferred_element_type=jnp.float32)
    total = lax.dot_general(gate_all, w_gate, contract_cols, preferred_element_type=jnp.float32)
    total = total + lax.dot_general(up_all, w_up, contract_cols, preferred_element_type=jnp.float32)
    model_width = out_part.shape[1]
    dealt = reduce_dealt(jnp.concatenate([out_part, total], axis=1), pick, n_fsdp)
    layer_out = dealt[:, :model_width]
    input_grad = dealt[:, model_width:]

    x_t = xall.T.astype(jnp.float32)
    keys_t = lax.dot_general(basis, keys_all, contract_cols, preferred_element_type=jnp.float32)
    xp_t = (x_t - keys_t).astype(jnp.bfloat16)
    grad_gate = jnp.dot(xp_t, gate_all, preferred_element_type=jnp.float32)
    grad_up = jnp.dot(xp_t, up_all, preferred_element_type=jnp.float32)
    return (layer_out, input_grad, grad_gate, grad_up, grad_down)


def solution(mesh):
    body = functools.partial(per_device, mesh.shape["dp"], mesh.shape["fsdp"])
    return jax.shard_map(
        body,
        mesh=mesh,
        in_specs=(
            P("fsdp", "dp"),
            P(),
            P(),
            P("dp", "fsdp"),
            P("dp", "fsdp"),
            P("fsdp", "dp"),
            P("dp", None),
            P("fsdp", "dp"),
        ),
        out_specs=(
            P("fsdp", "dp"),
            P("fsdp", "dp"),
            P("dp", "fsdp"),
            P("dp", "fsdp"),
            P("fsdp", "dp"),
        ),
        check_vma=False,
    )
```

```python
import functools

import jax
import jax.numpy as jnp
from jax import lax
from jax.sharding import PartitionSpec as P

MOST = 16


def deal_tables(doc_lengths, doc_dests):
    groups = doc_lengths.shape[0]
    starts = jnp.cumsum(doc_lengths, axis=1) - doc_lengths
    targets = jnp.arange(groups, dtype=jnp.int32)
    hits = (doc_dests[:, :, None] == targets[None, None, :]).astype(jnp.int32)
    loads = jnp.sum(doc_lengths[:, :, None] * hits, axis=1)
    firsts = jnp.sum(starts[:, :, None] * hits, axis=1)
    return (loads, firsts)


def token_rows(doc_lengths, doc_dests, loads, tok, recv):
    sources, ndoc = doc_lengths.shape
    starts = jnp.cumsum(doc_lengths, axis=1) - doc_lengths
    ends = starts + doc_lengths
    offsets = jnp.cumsum(loads, axis=0) - loads
    t = jnp.arange(tok, dtype=jnp.int32)
    doc_of = jnp.sum((ends[:, :, None] <= t[None, None, :]).astype(jnp.int32), axis=1)
    doc_of = jnp.minimum(doc_of, ndoc - 1)
    hit = (doc_of[:, :, None] == jnp.arange(ndoc, dtype=jnp.int32)[None, None, :]).astype(jnp.int32)
    dst = jnp.sum(hit * doc_dests[:, None, :], axis=2)
    st = jnp.sum(hit * starts[:, None, :], axis=2)
    to = (dst[:, :, None] == jnp.arange(sources, dtype=jnp.int32)[None, None, :]).astype(jnp.int32)
    off = jnp.sum(to * offsets[:, None, :], axis=2)
    row = dst * recv + off + t[None, :] - st
    return row.reshape(-1)


def settle(term):
    return lax.optimization_barrier(term.astype(jnp.bfloat16)).astype(jnp.float32)


def reduce_rows(part, axis, n):
    rows, cols = part.shape
    got = lax.all_to_all(part.astype(jnp.bfloat16).reshape(n, rows // n, cols), axis, 0, 0, tiled=True)
    return jnp.sum(got.astype(jnp.float32), axis=0)


def gather_rows(block, axis, n):
    rows, cols = block.shape
    got = lax.all_to_all(jnp.broadcast_to(block[None], (n, rows, cols)), axis, 0, 0, tiled=True)
    return got.reshape(n * rows, cols)


def reduce_dealt(part, pick, blocks):
    cols = part.shape[1]
    contract_rows = (((0,), (0,)), ((), ()))
    send = lax.dot_general(pick, part.astype(jnp.bfloat16), contract_rows, preferred_element_type=jnp.float32)
    send = send.astype(jnp.bfloat16).reshape(blocks, 2, -1, cols)
    odd = lax.axis_index("fsdp") % 2 == 1
    keep = jnp.where(odd, send[:, 1], send[:, 0])
    give = jnp.where(odd, send[:, 0], send[:, 1])
    got = lax.ppermute(give, "fsdp", [(f, f ^ 1) for f in range(blocks)])
    pair = (keep.astype(jnp.float32) + got.astype(jnp.float32)).astype(jnp.bfloat16)
    came = lax.all_to_all(pair, "fsdp", 0, 0, tiled=True)
    halves = jnp.sum(came.astype(jnp.float32).reshape(blocks // 2, 2, -1, cols), axis=0)
    return halves.reshape(-1, cols).astype(jnp.bfloat16)


def per_device(n_dp, n_fsdp, x_src, doc_lengths, doc_dests, w_gate, w_up, w_down, basis, out_cotangent):
    hidden_width = w_gate.shape[1]
    tok = x_src.shape[0]
    recv = out_cotangent.shape[0]
    loads, firsts = deal_tables(doc_lengths, doc_dests)
    rows_of = token_rows(doc_lengths, doc_dests, loads, tok, recv)
    dealt_rows = jnp.arange(n_fsdp * recv, dtype=jnp.int32)
    pick = (rows_of[:, None] == dealt_rows[None, :]).astype(jnp.bfloat16)
    contract_rows = (((0,), (0,)), ((), ()))
    contract_cols = (((1,), (1,)), ((), ()))

    xall = gather_rows(x_src, "fsdp", n_fsdp)
    dy_dealt = lax.all_gather(out_cotangent, "fsdp", axis=0, tiled=True)
    dyall = jnp.dot(pick, dy_dealt, preferred_element_type=jnp.float32).astype(jnp.bfloat16)
    first = jnp.dot(xall, w_gate, preferred_element_type=jnp.float32)
    second = jnp.dot(xall, w_up, preferred_element_type=jnp.float32)
    keys_local = jnp.dot(xall, basis, preferred_element_type=jnp.float32)
    both = reduce_rows(jnp.concatenate([first, second, keys_local], axis=1), "dp", n_dp)
    gate = both[:, :hidden_width]
    up = both[:, hidden_width:2 * hidden_width]
    keys = both[:, 2 * hidden_width:].astype(jnp.bfloat16)
    sig = jax.nn.sigmoid(gate)
    hidden = (gate * sig * up).astype(jnp.bfloat16)

    hg_part = lax.dot_general(dyall, w_down, contract_cols, preferred_element_type=jnp.float32)
    hidden_grad = reduce_rows(hg_part, "dp", n_dp)
    gate_grad = (hidden_grad * up * sig * (1.0 + gate * (1.0 - sig))).astype(jnp.bfloat16)
    up_grad = (hidden_grad * gate * sig).astype(jnp.bfloat16)
    gathered = gather_rows(jnp.concatenate([hidden, gate_grad, up_grad, keys], axis=1), "dp", n_dp)
    hall = gathered[:, :hidden_width]
    gate_all = gathered[:, hidden_width:2 * hidden_width]
    up_all = gathered[:, 2 * hidden_width:3 * hidden_width]
    keys_all = gathered[:, 3 * hidden_width:]
    out_part = jnp.dot(hall, w_down, preferred_element_type=jnp.float32)
    grad_down = lax.dot_general(hall, dyall, contract_rows, preferred_element_type=jnp.float32)
    total = lax.dot_general(gate_all, w_gate, contract_cols, preferred_element_type=jnp.float32)
    total = total + lax.dot_general(up_all, w_up, contract_cols, preferred_element_type=jnp.float32)
    model_width = out_part.shape[1]
    dealt = reduce_dealt(jnp.concatenate([out_part, total], axis=1), pick, n_fsdp)
    layer_out = dealt[:, :model_width]
    input_grad = dealt[:, model_width:]

    x_t = xall.T.astype(jnp.float32)
    keys_t = lax.dot_general(basis, keys_all, contract_cols, preferred_element_type=jnp.float32)
    xp_t = (x_t - keys_t).astype(jnp.bfloat16)
    grad_gate = jnp.dot(xp_t, gate_all, preferred_element_type=jnp.float32)
    grad_up = jnp.dot(xp_t, up_all, preferred_element_type=jnp.float32)
    return (layer_out, input_grad, grad_gate, grad_up, grad_down)


def solution(mesh):
    body = functools.partial(per_device, mesh.shape["dp"], mesh.shape["fsdp"])
    return jax.shard_map(
        body,
        mesh=mesh,
        in_specs=(
            P("fsdp", "dp"),
            P(),
            P(),
            P("dp", "fsdp"),
            P("dp", "fsdp"),
            P("fsdp", "dp"),
            P("dp", None),
            P("fsdp", "dp"),
        ),
        out_specs=(
            P("fsdp", "dp"),
            P("fsdp", "dp"),
            P("dp", "fsdp"),
            P("dp", "fsdp"),
            P("fsdp", "dp"),
        ),
        check_vma=False,
    )
```

```python
import functools

import jax
import jax.numpy as jnp
from jax import lax
from jax.sharding import PartitionSpec as P

MOST = 16


def deal_tables(doc_lengths, doc_dests):
    groups = doc_lengths.shape[0]
    starts = jnp.cumsum(doc_lengths, axis=1) - doc_lengths
    targets = jnp.arange(groups, dtype=jnp.int32)
    hits = (doc_dests[:, :, None] == targets[None, None, :]).astype(jnp.int32)
    loads = jnp.sum(doc_lengths[:, :, None] * hits, axis=1)
    firsts = jnp.sum(starts[:, :, None] * hits, axis=1)
    return (loads, firsts)


def token_rows(doc_lengths, doc_dests, loads, tok, recv):
    sources, ndoc = doc_lengths.shape
    starts = jnp.cumsum(doc_lengths, axis=1) - doc_lengths
    ends = starts + doc_lengths
    offsets = jnp.cumsum(loads, axis=0) - loads
    t = jnp.arange(tok, dtype=jnp.int32)
    doc_of = jnp.sum((ends[:, :, None] <= t[None, None, :]).astype(jnp.int32), axis=1)
    doc_of = jnp.minimum(doc_of, ndoc - 1)
    hit = (doc_of[:, :, None] == jnp.arange(ndoc, dtype=jnp.int32)[None, None, :]).astype(jnp.int32)
    dst = jnp.sum(hit * doc_dests[:, None, :], axis=2)
    st = jnp.sum(hit * starts[:, None, :], axis=2)
    to = (dst[:, :, None] == jnp.arange(sources, dtype=jnp.int32)[None, None, :]).astype(jnp.int32)
    off = jnp.sum(to * offsets[:, None, :], axis=2)
    row = dst * recv + off + t[None, :] - st
    return row.reshape(-1)


def settle(term):
    return lax.optimization_barrier(term.astype(jnp.bfloat16)).astype(jnp.float32)


def reduce_rows(part, axis, n):
    rows, cols = part.shape
    got = lax.all_to_all(part.astype(jnp.bfloat16).reshape(n, rows // n, cols), axis, 0, 0, tiled=True)
    return jnp.sum(got.astype(jnp.float32), axis=0)


def gather_rows(block, axis, n):
    rows, cols = block.shape
    got = lax.all_to_all(jnp.broadcast_to(block[None], (n, rows, cols)), axis, 0, 0, tiled=True)
    return got.reshape(n * rows, cols)


def reduce_dealt(part, pick, blocks):
    cols = part.shape[1]
    contract_rows = (((0,), (0,)), ((), ()))
    send = lax.dot_general(pick, part.astype(jnp.bfloat16), contract_rows, preferred_element_type=jnp.float32)
    send = send.astype(jnp.bfloat16).reshape(blocks, 2, -1, cols)
    odd = lax.axis_index("fsdp") % 2 == 1
    keep = jnp.where(odd, send[:, 1], send[:, 0])
    give = jnp.where(odd, send[:, 0], send[:, 1])
    got = lax.ppermute(give, "fsdp", [(f, f ^ 1) for f in range(blocks)])
    pair = (keep.astype(jnp.float32) + got.astype(jnp.float32)).astype(jnp.bfloat16)
    came = lax.all_to_all(pair, "fsdp", 0, 0, tiled=True)
    halves = jnp.sum(came.astype(jnp.float32).reshape(blocks // 2, 2, -1, cols), axis=0)
    return halves.reshape(-1, cols).astype(jnp.bfloat16)


def per_device(n_dp, n_fsdp, x_src, doc_lengths, doc_dests, w_gate, w_up, w_down, basis, out_cotangent):
    hidden_width = w_gate.shape[1]
    tok = x_src.shape[0]
    recv = out_cotangent.shape[0]
    loads, firsts = deal_tables(doc_lengths, doc_dests)
    rows_of = token_rows(doc_lengths, doc_dests, loads, tok, recv)
    dealt_rows = jnp.arange(n_fsdp * recv, dtype=jnp.int32)
    pick = (rows_of[:, None] == dealt_rows[None, :]).astype(jnp.bfloat16)
    contract_rows = (((0,), (0,)), ((), ()))
    contract_cols = (((1,), (1,)), ((), ()))

    half_x = tok // 2
    half_dy = recv // 2
    halves = jnp.stack([
        jnp.concatenate([x_src[:half_x], out_cotangent[:half_dy]], axis=0),
        jnp.concatenate([x_src[half_x:], out_cotangent[half_dy:]], axis=0),
    ])
    came = lax.all_to_all(jnp.tile(halves, (n_fsdp // 2, 1, 1)), "fsdp", 0, 0, tiled=True)
    other = lax.ppermute(came, "fsdp", [(f, f ^ 1) for f in range(n_fsdp)])
    odd = lax.axis_index("fsdp") % 2 == 1
    low = jnp.where(odd, other, came)
    high = jnp.where(odd, came, other)
    xall = jnp.concatenate([low[:, :half_x], high[:, :half_x]], axis=1).reshape(-1, x_src.shape[1])
    dy_dealt = jnp.concatenate([low[:, half_x:], high[:, half_x:]], axis=1).reshape(-1, x_src.shape[1])
    dyall = jnp.dot(pick, dy_dealt, preferred_element_type=jnp.float32).astype(jnp.bfloat16)
    first = jnp.dot(xall, w_gate, preferred_element_type=jnp.float32)
    second = jnp.dot(xall, w_up, preferred_element_type=jnp.float32)
    keys_local = jnp.dot(xall, basis, preferred_element_type=jnp.float32)
    both = reduce_rows(jnp.concatenate([first, second, keys_local], axis=1), "dp", n_dp)
    gate = both[:, :hidden_width]
    up = both[:, hidden_width:2 * hidden_width]
    keys = both[:, 2 * hidden_width:].astype(jnp.bfloat16)
    sig = jax.nn.sigmoid(gate)
    hidden = (gate * sig * up).astype(jnp.bfloat16)

    hg_part = lax.dot_general(dyall, w_down, contract_cols, preferred_element_type=jnp.float32)
    hidden_grad = reduce_rows(hg_part, "dp", n_dp)
    gate_grad = (hidden_grad * up * sig * (1.0 + gate * (1.0 - sig))).astype(jnp.bfloat16)
    up_grad = (hidden_grad * gate * sig).astype(jnp.bfloat16)
    gathered = gather_rows(jnp.concatenate([hidden, gate_grad, up_grad, keys], axis=1), "dp", n_dp)
    hall = gathered[:, :hidden_width]
    gate_all = gathered[:, hidden_width:2 * hidden_width]
    up_all = gathered[:, 2 * hidden_width:3 * hidden_width]
    keys_all = gathered[:, 3 * hidden_width:]
    out_part = jnp.dot(hall, w_down, preferred_element_type=jnp.float32)
    grad_down = lax.dot_general(hall, dyall, contract_rows, preferred_element_type=jnp.float32)
    total = lax.dot_general(gate_all, w_gate, contract_cols, preferred_element_type=jnp.float32)
    total = total + lax.dot_general(up_all, w_up, contract_cols, preferred_element_type=jnp.float32)
    model_width = out_part.shape[1]
    dealt = reduce_dealt(jnp.concatenate([out_part, total], axis=1), pick, n_fsdp)
    layer_out = dealt[:, :model_width]
    input_grad = dealt[:, model_width:]

    x_t = xall.T.astype(jnp.float32)
    keys_t = lax.dot_general(basis, keys_all, contract_cols, preferred_element_type=jnp.float32)
    xp_t = (x_t - keys_t).astype(jnp.bfloat16)
    grad_gate = jnp.dot(xp_t, gate_all, preferred_element_type=jnp.float32)
    grad_up = jnp.dot(xp_t, up_all, preferred_element_type=jnp.float32)
    return (layer_out, input_grad, grad_gate, grad_up, grad_down)


def solution(mesh):
    body = functools.partial(per_device, mesh.shape["dp"], mesh.shape["fsdp"])
    return jax.shard_map(
        body,
        mesh=mesh,
        in_specs=(
            P("fsdp", "dp"),
            P(),
            P(),
            P("dp", "fsdp"),
            P("dp", "fsdp"),
            P("fsdp", "dp"),
            P("dp", None),
            P("fsdp", "dp"),
        ),
        out_specs=(
            P("fsdp", "dp"),
            P("fsdp", "dp"),
            P("dp", "fsdp"),
            P("dp", "fsdp"),
            P("fsdp", "dp"),
        ),
        check_vma=False,
    )
```

```python
import functools

import jax
import jax.numpy as jnp
from jax import lax
from jax.sharding import PartitionSpec as P

MOST = 16


def deal_tables(doc_lengths, doc_dests):
    groups = doc_lengths.shape[0]
    starts = jnp.cumsum(doc_lengths, axis=1) - doc_lengths
    targets = jnp.arange(groups, dtype=jnp.int32)
    hits = (doc_dests[:, :, None] == targets[None, None, :]).astype(jnp.int32)
    loads = jnp.sum(doc_lengths[:, :, None] * hits, axis=1)
    firsts = jnp.sum(starts[:, :, None] * hits, axis=1)
    return (loads, firsts)


def token_rows(doc_lengths, doc_dests, loads, tok, recv):
    sources, ndoc = doc_lengths.shape
    starts = jnp.cumsum(doc_lengths, axis=1) - doc_lengths
    ends = starts + doc_lengths
    offsets = jnp.cumsum(loads, axis=0) - loads
    t = jnp.arange(tok, dtype=jnp.int32)
    doc_of = jnp.sum((ends[:, :, None] <= t[None, None, :]).astype(jnp.int32), axis=1)
    doc_of = jnp.minimum(doc_of, ndoc - 1)
    hit = (doc_of[:, :, None] == jnp.arange(ndoc, dtype=jnp.int32)[None, None, :]).astype(jnp.int32)
    dst = jnp.sum(hit * doc_dests[:, None, :], axis=2)
    st = jnp.sum(hit * starts[:, None, :], axis=2)
    to = (dst[:, :, None] == jnp.arange(sources, dtype=jnp.int32)[None, None, :]).astype(jnp.int32)
    off = jnp.sum(to * offsets[:, None, :], axis=2)
    row = dst * recv + off + t[None, :] - st
    return row.reshape(-1)


def settle(term):
    return lax.optimization_barrier(term.astype(jnp.bfloat16)).astype(jnp.float32)


def reduce_rows(part, axis, n):
    rows, cols = part.shape
    got = lax.all_to_all(part.astype(jnp.bfloat16).reshape(n, rows // n, cols), axis, 0, 0, tiled=True)
    return jnp.sum(got.astype(jnp.float32), axis=0)


def gather_rows(block, axis, n):
    rows, cols = block.shape
    got = lax.all_to_all(jnp.broadcast_to(block[None], (n, rows, cols)), axis, 0, 0, tiled=True)
    return got.reshape(n * rows, cols)


def reduce_dealt(part, pick, blocks):
    cols = part.shape[1]
    contract_rows = (((0,), (0,)), ((), ()))
    send = lax.dot_general(pick, part.astype(jnp.bfloat16), contract_rows, preferred_element_type=jnp.float32)
    send = send.astype(jnp.bfloat16).reshape(blocks, 2, -1, cols)
    odd = lax.axis_index("fsdp") % 2 == 1
    keep = jnp.where(odd, send[:, 1], send[:, 0])
    give = jnp.where(odd, send[:, 0], send[:, 1])
    got = lax.ppermute(give, "fsdp", [(f, f ^ 1) for f in range(blocks)])
    pair = (keep.astype(jnp.float32) + got.astype(jnp.float32)).astype(jnp.bfloat16)
    came = lax.all_to_all(pair, "fsdp", 0, 0, tiled=True)
    halves = jnp.sum(came.astype(jnp.float32).reshape(blocks // 2, 2, -1, cols), axis=0)
    return halves.reshape(-1, cols).astype(jnp.bfloat16)


def per_device(n_dp, n_fsdp, x_src, doc_lengths, doc_dests, w_gate, w_up, w_down, basis, out_cotangent):
    hidden_width = w_gate.shape[1]
    tok = x_src.shape[0]
    recv = out_cotangent.shape[0]
    loads, firsts = deal_tables(doc_lengths, doc_dests)
    rows_of = token_rows(doc_lengths, doc_dests, loads, tok, recv)
    dealt_rows = jnp.arange(n_fsdp * recv, dtype=jnp.int32)
    pick = (rows_of[:, None] == dealt_rows[None, :]).astype(jnp.bfloat16)
    contract_rows = (((0,), (0,)), ((), ()))
    contract_cols = (((1,), (1,)), ((), ()))

    half_x = tok // 2
    half_dy = recv // 2
    halves = jnp.stack([
        jnp.concatenate([x_src[:half_x], out_cotangent[:half_dy]], axis=0),
        jnp.concatenate([x_src[half_x:], out_cotangent[half_dy:]], axis=0),
    ])
    came = lax.all_to_all(jnp.tile(halves, (n_fsdp // 2, 1, 1)), "fsdp", 0, 0, tiled=True)
    other = lax.ppermute(came, "fsdp", [(f, f ^ 1) for f in range(n_fsdp)])
    odd = lax.axis_index("fsdp") % 2 == 1
    low = jnp.where(odd, other, came)
    high = jnp.where(odd, came, other)
    xall = jnp.concatenate([low[:, :half_x], high[:, :half_x]], axis=1).reshape(-1, x_src.shape[1])
    dy_dealt = jnp.concatenate([low[:, half_x:], high[:, half_x:]], axis=1).reshape(-1, x_src.shape[1])
    dyall = jnp.dot(pick, dy_dealt, preferred_element_type=jnp.float32).astype(jnp.bfloat16)
    first = jnp.dot(xall, w_gate, preferred_element_type=jnp.float32)
    second = jnp.dot(xall, w_up, preferred_element_type=jnp.float32)
    key_half = basis.shape[1] // 2
    basis_half = lax.dynamic_slice_in_dim(basis, (lax.axis_index("fsdp") % 2) * key_half, key_half, 1)
    keys_local = jnp.dot(xall, basis_half, preferred_element_type=jnp.float32)
    both = reduce_rows(jnp.concatenate([first, second, keys_local], axis=1), "dp", n_dp)
    gate = both[:, :hidden_width]
    up = both[:, hidden_width:2 * hidden_width]
    keys = both[:, 2 * hidden_width:].astype(jnp.bfloat16)
    sig = jax.nn.sigmoid(gate)
    hidden = (gate * sig * up).astype(jnp.bfloat16)

    hg_part = lax.dot_general(dyall, w_down, contract_cols, preferred_element_type=jnp.float32)
    hidden_grad = reduce_rows(hg_part, "dp", n_dp)
    gate_grad = (hidden_grad * up * sig * (1.0 + gate * (1.0 - sig))).astype(jnp.bfloat16)
    up_grad = (hidden_grad * gate * sig).astype(jnp.bfloat16)
    gathered = gather_rows(jnp.concatenate([hidden, gate_grad, up_grad, keys], axis=1), "dp", n_dp)
    hall = gathered[:, :hidden_width]
    gate_all = gathered[:, hidden_width:2 * hidden_width]
    up_all = gathered[:, 2 * hidden_width:3 * hidden_width]
    keys_mine = gathered[:, 3 * hidden_width:]
    keys_other = lax.ppermute(keys_mine, "fsdp", [(f, f ^ 1) for f in range(n_fsdp)])
    keys_all = jnp.where(
        odd,
        jnp.concatenate([keys_other, keys_mine], axis=1),
        jnp.concatenate([keys_mine, keys_other], axis=1),
    )
    out_part = jnp.dot(hall, w_down, preferred_element_type=jnp.float32)
    grad_down = lax.dot_general(hall, dyall, contract_rows, preferred_element_type=jnp.float32)
    total = lax.dot_general(gate_all, w_gate, contract_cols, preferred_element_type=jnp.float32)
    total = total + lax.dot_general(up_all, w_up, contract_cols, preferred_element_type=jnp.float32)
    model_width = out_part.shape[1]
    dealt = reduce_dealt(jnp.concatenate([out_part, total], axis=1), pick, n_fsdp)
    layer_out = dealt[:, :model_width]
    input_grad = dealt[:, model_width:]

    x_t = xall.T.astype(jnp.float32)
    keys_t = lax.dot_general(basis, keys_all, contract_cols, preferred_element_type=jnp.float32)
    xp_t = (x_t - keys_t).astype(jnp.bfloat16)
    grad_gate = jnp.dot(xp_t, gate_all, preferred_element_type=jnp.float32)
    grad_up = jnp.dot(xp_t, up_all, preferred_element_type=jnp.float32)
    return (layer_out, input_grad, grad_gate, grad_up, grad_down)


def solution(mesh):
    body = functools.partial(per_device, mesh.shape["dp"], mesh.shape["fsdp"])
    return jax.shard_map(
        body,
        mesh=mesh,
        in_specs=(
            P("fsdp", "dp"),
            P(),
            P(),
            P("dp", "fsdp"),
            P("dp", "fsdp"),
            P("fsdp", "dp"),
            P("dp", None),
            P("fsdp", "dp"),
        ),
        out_specs=(
            P("fsdp", "dp"),
            P("fsdp", "dp"),
            P("dp", "fsdp"),
            P("dp", "fsdp"),
            P("fsdp", "dp"),
        ),
        check_vma=False,
    )
```

```python
import functools

import jax
import jax.numpy as jnp
from jax import lax
from jax.sharding import PartitionSpec as P

MOST = 16


def deal_tables(doc_lengths, doc_dests):
    groups = doc_lengths.shape[0]
    starts = jnp.cumsum(doc_lengths, axis=1) - doc_lengths
    targets = jnp.arange(groups, dtype=jnp.int32)
    hits = (doc_dests[:, :, None] == targets[None, None, :]).astype(jnp.int32)
    loads = jnp.sum(doc_lengths[:, :, None] * hits, axis=1)
    firsts = jnp.sum(starts[:, :, None] * hits, axis=1)
    return (loads, firsts)


def token_rows(doc_lengths, doc_dests, loads, tok, recv):
    sources, ndoc = doc_lengths.shape
    starts = jnp.cumsum(doc_lengths, axis=1) - doc_lengths
    ends = starts + doc_lengths
    offsets = jnp.cumsum(loads, axis=0) - loads
    t = jnp.arange(tok, dtype=jnp.int32)
    doc_of = jnp.sum((ends[:, :, None] <= t[None, None, :]).astype(jnp.int32), axis=1)
    doc_of = jnp.minimum(doc_of, ndoc - 1)
    hit = (doc_of[:, :, None] == jnp.arange(ndoc, dtype=jnp.int32)[None, None, :]).astype(jnp.int32)
    dst = jnp.sum(hit * doc_dests[:, None, :], axis=2)
    st = jnp.sum(hit * starts[:, None, :], axis=2)
    to = (dst[:, :, None] == jnp.arange(sources, dtype=jnp.int32)[None, None, :]).astype(jnp.int32)
    off = jnp.sum(to * offsets[:, None, :], axis=2)
    row = dst * recv + off + t[None, :] - st
    return row.reshape(-1)


def settle(term):
    return lax.optimization_barrier(term.astype(jnp.bfloat16)).astype(jnp.float32)


def reduce_rows(part, axis, n):
    rows, cols = part.shape
    got = lax.all_to_all(part.astype(jnp.bfloat16).reshape(n, rows // n, cols), axis, 0, 0, tiled=True)
    return jnp.sum(got.astype(jnp.float32), axis=0)


def gather_rows(block, axis, n):
    rows, cols = block.shape
    got = lax.all_to_all(jnp.broadcast_to(block[None], (n, rows, cols)), axis, 0, 0, tiled=True)
    return got.reshape(n * rows, cols)


def reduce_dealt(part, pick, blocks):
    cols = part.shape[1]
    contract_rows = (((0,), (0,)), ((), ()))
    send = lax.dot_general(pick, part.astype(jnp.bfloat16), contract_rows, preferred_element_type=jnp.float32)
    send = send.astype(jnp.bfloat16).reshape(blocks, 2, -1, cols)
    odd = lax.axis_index("fsdp") % 2 == 1
    keep = jnp.where(odd, send[:, 1], send[:, 0])
    give = jnp.where(odd, send[:, 0], send[:, 1])
    got = lax.ppermute(give, "fsdp", [(f, f ^ 1) for f in range(blocks)])
    pair = (keep.astype(jnp.float32) + got.astype(jnp.float32)).astype(jnp.bfloat16)
    came = lax.all_to_all(pair, "fsdp", 0, 0, tiled=True)
    halves = jnp.sum(came.astype(jnp.float32).reshape(blocks // 2, 2, -1, cols), axis=0)
    return halves.reshape(-1, cols).astype(jnp.bfloat16)


def per_device(n_dp, n_fsdp, x_src, doc_lengths, doc_dests, w_gate, w_up, w_down, basis, out_cotangent):
    hidden_width = w_gate.shape[1]
    tok = x_src.shape[0]
    recv = out_cotangent.shape[0]
    loads, firsts = deal_tables(doc_lengths, doc_dests)
    rows_of = token_rows(doc_lengths, doc_dests, loads, tok, recv)
    dealt_rows = jnp.arange(n_fsdp * recv, dtype=jnp.int32)
    pick = (rows_of[:, None] == dealt_rows[None, :]).astype(jnp.bfloat16)
    contract_rows = (((0,), (0,)), ((), ()))
    contract_cols = (((1,), (1,)), ((), ()))

    half_x = tok // 2
    half_dy = recv // 2
    halves = jnp.stack([
        jnp.concatenate([x_src[:half_x], out_cotangent[:half_dy]], axis=0),
        jnp.concatenate([x_src[half_x:], out_cotangent[half_dy:]], axis=0),
    ])
    came = lax.all_to_all(jnp.tile(halves, (n_fsdp // 2, 1, 1)), "fsdp", 0, 0, tiled=True)
    other = lax.ppermute(came, "fsdp", [(f, f ^ 1) for f in range(n_fsdp)])
    odd = lax.axis_index("fsdp") % 2 == 1
    low = jnp.where(odd, other, came)
    high = jnp.where(odd, came, other)
    xall = jnp.concatenate([low[:, :half_x], high[:, :half_x]], axis=1).reshape(-1, x_src.shape[1])
    dy_dealt = jnp.concatenate([low[:, half_x:], high[:, half_x:]], axis=1).reshape(-1, x_src.shape[1])
    dyall = jnp.dot(pick, dy_dealt, preferred_element_type=jnp.float32).astype(jnp.bfloat16)
    first = jnp.dot(xall, w_gate, preferred_element_type=jnp.float32)
    second = jnp.dot(xall, w_up, preferred_element_type=jnp.float32)
    key_half = basis.shape[1] // 2
    basis_half = lax.dynamic_slice_in_dim(basis, (lax.axis_index("fsdp") % 2) * key_half, key_half, 1)
    keys_local = jnp.dot(xall, basis_half, preferred_element_type=jnp.float32)
    hg_part = lax.dot_general(dyall, w_down, contract_cols, preferred_element_type=jnp.float32)
    both = reduce_rows(jnp.concatenate([first, second, keys_local, hg_part], axis=1), "dp", n_dp)
    gate = both[:, :hidden_width]
    up = both[:, hidden_width:2 * hidden_width]
    keys = both[:, 2 * hidden_width:2 * hidden_width + key_half].astype(jnp.bfloat16)
    hidden_grad = both[:, 2 * hidden_width + key_half:]
    sig = jax.nn.sigmoid(gate)
    hidden = (gate * sig * up).astype(jnp.bfloat16)

    gate_grad = (hidden_grad * up * sig * (1.0 + gate * (1.0 - sig))).astype(jnp.bfloat16)
    up_grad = (hidden_grad * gate * sig).astype(jnp.bfloat16)
    gathered = gather_rows(jnp.concatenate([hidden, gate_grad, up_grad, keys], axis=1), "dp", n_dp)
    hall = gathered[:, :hidden_width]
    gate_all = gathered[:, hidden_width:2 * hidden_width]
    up_all = gathered[:, 2 * hidden_width:3 * hidden_width]
    keys_mine = gathered[:, 3 * hidden_width:]
    keys_other = lax.ppermute(keys_mine, "fsdp", [(f, f ^ 1) for f in range(n_fsdp)])
    keys_all = jnp.where(
        odd,
        jnp.concatenate([keys_other, keys_mine], axis=1),
        jnp.concatenate([keys_mine, keys_other], axis=1),
    )
    out_part = jnp.dot(hall, w_down, preferred_element_type=jnp.float32)
    grad_down = lax.dot_general(hall, dyall, contract_rows, preferred_element_type=jnp.float32)
    total = lax.dot_general(gate_all, w_gate, contract_cols, preferred_element_type=jnp.float32)
    total = total + lax.dot_general(up_all, w_up, contract_cols, preferred_element_type=jnp.float32)
    model_width = out_part.shape[1]
    dealt = reduce_dealt(jnp.concatenate([out_part, total], axis=1), pick, n_fsdp)
    layer_out = dealt[:, :model_width]
    input_grad = dealt[:, model_width:]

    x_t = xall.T.astype(jnp.float32)
    keys_t = lax.dot_general(basis, keys_all, contract_cols, preferred_element_type=jnp.float32)
    xp_t = (x_t - keys_t).astype(jnp.bfloat16)
    grad_gate = jnp.dot(xp_t, gate_all, preferred_element_type=jnp.float32)
    grad_up = jnp.dot(xp_t, up_all, preferred_element_type=jnp.float32)
    return (layer_out, input_grad, grad_gate, grad_up, grad_down)


def solution(mesh):
    body = functools.partial(per_device, mesh.shape["dp"], mesh.shape["fsdp"])
    return jax.shard_map(
        body,
        mesh=mesh,
        in_specs=(
            P("fsdp", "dp"),
            P(),
            P(),
            P("dp", "fsdp"),
            P("dp", "fsdp"),
            P("fsdp", "dp"),
            P("dp", None),
            P("fsdp", "dp"),
        ),
        out_specs=(
            P("fsdp", "dp"),
            P("fsdp", "dp"),
            P("dp", "fsdp"),
            P("dp", "fsdp"),
            P("fsdp", "dp"),
        ),
        check_vma=False,
    )
```

```python
import functools

import jax
import jax.numpy as jnp
from jax import lax
from jax.sharding import PartitionSpec as P

MOST = 16


def deal_tables(doc_lengths, doc_dests):
    groups = doc_lengths.shape[0]
    starts = jnp.cumsum(doc_lengths, axis=1) - doc_lengths
    targets = jnp.arange(groups, dtype=jnp.int32)
    hits = (doc_dests[:, :, None] == targets[None, None, :]).astype(jnp.int32)
    loads = jnp.sum(doc_lengths[:, :, None] * hits, axis=1)
    firsts = jnp.sum(starts[:, :, None] * hits, axis=1)
    return (loads, firsts)


def token_rows(doc_lengths, doc_dests, loads, tok, recv):
    sources, ndoc = doc_lengths.shape
    starts = jnp.cumsum(doc_lengths, axis=1) - doc_lengths
    ends = starts + doc_lengths
    offsets = jnp.cumsum(loads, axis=0) - loads
    t = jnp.arange(tok, dtype=jnp.int32)
    doc_of = jnp.sum((ends[:, :, None] <= t[None, None, :]).astype(jnp.int32), axis=1)
    doc_of = jnp.minimum(doc_of, ndoc - 1)
    hit = (doc_of[:, :, None] == jnp.arange(ndoc, dtype=jnp.int32)[None, None, :]).astype(jnp.int32)
    dst = jnp.sum(hit * doc_dests[:, None, :], axis=2)
    st = jnp.sum(hit * starts[:, None, :], axis=2)
    to = (dst[:, :, None] == jnp.arange(sources, dtype=jnp.int32)[None, None, :]).astype(jnp.int32)
    off = jnp.sum(to * offsets[:, None, :], axis=2)
    row = dst * recv + off + t[None, :] - st
    return row.reshape(-1)


def settle(term):
    return lax.optimization_barrier(term.astype(jnp.bfloat16)).astype(jnp.float32)


def reduce_rows(part, axis, n):
    rows, cols = part.shape
    got = lax.all_to_all(part.astype(jnp.bfloat16).reshape(n, rows // n, cols), axis, 0, 0, tiled=True)
    return jnp.sum(got.astype(jnp.float32), axis=0)


def reduce_rows_permuted(part, axis, n):
    rows, cols = part.shape
    blocks = part.astype(jnp.bfloat16).reshape(n, rows // n, cols)
    me = lax.axis_index(axis)
    total = lax.dynamic_index_in_dim(blocks, me, 0, keepdims=False).astype(jnp.float32)
    for k in range(1, n):
        chunk = lax.dynamic_index_in_dim(blocks, (me + k) % n, 0, keepdims=False)
        moved = lax.ppermute(chunk, axis, [(i, (i + k) % n) for i in range(n)])
        total = total + moved.astype(jnp.float32)
    return total


def gather_rows(block, axis, n):
    rows, cols = block.shape
    got = lax.all_to_all(jnp.broadcast_to(block[None], (n, rows, cols)), axis, 0, 0, tiled=True)
    return got.reshape(n * rows, cols)


def reduce_dealt(part, pick, blocks):
    cols = part.shape[1]
    contract_rows = (((0,), (0,)), ((), ()))
    send = lax.dot_general(pick, part.astype(jnp.bfloat16), contract_rows, preferred_element_type=jnp.float32)
    send = send.astype(jnp.bfloat16).reshape(blocks, 2, -1, cols)
    odd = lax.axis_index("fsdp") % 2 == 1
    keep = jnp.where(odd, send[:, 1], send[:, 0])
    give = jnp.where(odd, send[:, 0], send[:, 1])
    got = lax.ppermute(give, "fsdp", [(f, f ^ 1) for f in range(blocks)])
    pair = (keep.astype(jnp.float32) + got.astype(jnp.float32)).astype(jnp.bfloat16)
    came = lax.all_to_all(pair, "fsdp", 0, 0, tiled=True)
    halves = jnp.sum(came.astype(jnp.float32).reshape(blocks // 2, 2, -1, cols), axis=0)
    return halves.reshape(-1, cols).astype(jnp.bfloat16)


def per_device(n_dp, n_fsdp, x_src, doc_lengths, doc_dests, w_gate, w_up, w_down, basis, out_cotangent):
    hidden_width = w_gate.shape[1]
    tok = x_src.shape[0]
    recv = out_cotangent.shape[0]
    loads, firsts = deal_tables(doc_lengths, doc_dests)
    rows_of = token_rows(doc_lengths, doc_dests, loads, tok, recv)
    dealt_rows = jnp.arange(n_fsdp * recv, dtype=jnp.int32)
    pick = (rows_of[:, None] == dealt_rows[None, :]).astype(jnp.bfloat16)
    contract_rows = (((0,), (0,)), ((), ()))
    contract_cols = (((1,), (1,)), ((), ()))

    half_x = tok // 2
    half_dy = recv // 2
    halves = jnp.stack([
        jnp.concatenate([x_src[:half_x], out_cotangent[:half_dy]], axis=0),
        jnp.concatenate([x_src[half_x:], out_cotangent[half_dy:]], axis=0),
    ])
    came = lax.all_to_all(jnp.tile(halves, (n_fsdp // 2, 1, 1)), "fsdp", 0, 0, tiled=True)
    other = lax.ppermute(came, "fsdp", [(f, f ^ 1) for f in range(n_fsdp)])
    odd = lax.axis_index("fsdp") % 2 == 1
    low = jnp.where(odd, other, came)
    high = jnp.where(odd, came, other)
    xall = jnp.concatenate([low[:, :half_x], high[:, :half_x]], axis=1).reshape(-1, x_src.shape[1])
    dy_dealt = jnp.concatenate([low[:, half_x:], high[:, half_x:]], axis=1).reshape(-1, x_src.shape[1])
    dyall = jnp.dot(pick, dy_dealt, preferred_element_type=jnp.float32).astype(jnp.bfloat16)
    first = jnp.dot(xall, w_gate, preferred_element_type=jnp.float32)
    second = jnp.dot(xall, w_up, preferred_element_type=jnp.float32)
    key_half = basis.shape[1] // 2
    basis_half = lax.dynamic_slice_in_dim(basis, (lax.axis_index("fsdp") % 2) * key_half, key_half, 1)
    keys_local = jnp.dot(xall, basis_half, preferred_element_type=jnp.float32)
    hg_part = lax.dot_general(dyall, w_down, contract_cols, preferred_element_type=jnp.float32)
    hidden_grad = reduce_rows_permuted(hg_part, "dp", n_dp)
    both = reduce_rows(jnp.concatenate([first, second, keys_local], axis=1), "dp", n_dp)
    gate = both[:, :hidden_width]
    up = both[:, hidden_width:2 * hidden_width]
    keys = both[:, 2 * hidden_width:].astype(jnp.bfloat16)
    sig = jax.nn.sigmoid(gate)
    hidden = (gate * sig * up).astype(jnp.bfloat16)

    gate_grad = (hidden_grad * up * sig * (1.0 + gate * (1.0 - sig))).astype(jnp.bfloat16)
    up_grad = (hidden_grad * gate * sig).astype(jnp.bfloat16)
    gathered = gather_rows(jnp.concatenate([hidden, gate_grad, up_grad, keys], axis=1), "dp", n_dp)
    hall = gathered[:, :hidden_width]
    gate_all = gathered[:, hidden_width:2 * hidden_width]
    up_all = gathered[:, 2 * hidden_width:3 * hidden_width]
    keys_mine = gathered[:, 3 * hidden_width:]
    keys_other = lax.ppermute(keys_mine, "fsdp", [(f, f ^ 1) for f in range(n_fsdp)])
    keys_all = jnp.where(
        odd,
        jnp.concatenate([keys_other, keys_mine], axis=1),
        jnp.concatenate([keys_mine, keys_other], axis=1),
    )
    out_part = jnp.dot(hall, w_down, preferred_element_type=jnp.float32)
    grad_down = lax.dot_general(hall, dyall, contract_rows, preferred_element_type=jnp.float32)
    total = lax.dot_general(gate_all, w_gate, contract_cols, preferred_element_type=jnp.float32)
    total = total + lax.dot_general(up_all, w_up, contract_cols, preferred_element_type=jnp.float32)
    model_width = out_part.shape[1]
    dealt = reduce_dealt(jnp.concatenate([out_part, total], axis=1), pick, n_fsdp)
    layer_out = dealt[:, :model_width]
    input_grad = dealt[:, model_width:]

    x_t = xall.T.astype(jnp.float32)
    keys_t = lax.dot_general(basis, keys_all, contract_cols, preferred_element_type=jnp.float32)
    xp_t = (x_t - keys_t).astype(jnp.bfloat16)
    grad_gate = jnp.dot(xp_t, gate_all, preferred_element_type=jnp.float32)
    grad_up = jnp.dot(xp_t, up_all, preferred_element_type=jnp.float32)
    return (layer_out, input_grad, grad_gate, grad_up, grad_down)


def solution(mesh):
    body = functools.partial(per_device, mesh.shape["dp"], mesh.shape["fsdp"])
    return jax.shard_map(
        body,
        mesh=mesh,
        in_specs=(
            P("fsdp", "dp"),
            P(),
            P(),
            P("dp", "fsdp"),
            P("dp", "fsdp"),
            P("fsdp", "dp"),
            P("dp", None),
            P("fsdp", "dp"),
        ),
        out_specs=(
            P("fsdp", "dp"),
            P("fsdp", "dp"),
            P("dp", "fsdp"),
            P("dp", "fsdp"),
            P("fsdp", "dp"),
        ),
        check_vma=False,
    )
```

```python
import functools

import jax
import jax.numpy as jnp
from jax import lax
from jax.sharding import PartitionSpec as P

MOST = 16


def deal_tables(doc_lengths, doc_dests):
    groups = doc_lengths.shape[0]
    starts = jnp.cumsum(doc_lengths, axis=1) - doc_lengths
    targets = jnp.arange(groups, dtype=jnp.int32)
    hits = (doc_dests[:, :, None] == targets[None, None, :]).astype(jnp.int32)
    loads = jnp.sum(doc_lengths[:, :, None] * hits, axis=1)
    firsts = jnp.sum(starts[:, :, None] * hits, axis=1)
    return (loads, firsts)


def token_rows(doc_lengths, doc_dests, loads, tok, recv):
    sources, ndoc = doc_lengths.shape
    starts = jnp.cumsum(doc_lengths, axis=1) - doc_lengths
    ends = starts + doc_lengths
    offsets = jnp.cumsum(loads, axis=0) - loads
    t = jnp.arange(tok, dtype=jnp.int32)
    doc_of = jnp.sum((ends[:, :, None] <= t[None, None, :]).astype(jnp.int32), axis=1)
    doc_of = jnp.minimum(doc_of, ndoc - 1)
    hit = (doc_of[:, :, None] == jnp.arange(ndoc, dtype=jnp.int32)[None, None, :]).astype(jnp.int32)
    dst = jnp.sum(hit * doc_dests[:, None, :], axis=2)
    st = jnp.sum(hit * starts[:, None, :], axis=2)
    to = (dst[:, :, None] == jnp.arange(sources, dtype=jnp.int32)[None, None, :]).astype(jnp.int32)
    off = jnp.sum(to * offsets[:, None, :], axis=2)
    row = dst * recv + off + t[None, :] - st
    return row.reshape(-1)


def settle(term):
    return lax.optimization_barrier(term.astype(jnp.bfloat16)).astype(jnp.float32)


def reduce_rows(part, axis, n):
    rows, cols = part.shape
    got = lax.all_to_all(part.astype(jnp.bfloat16).reshape(n, rows // n, cols), axis, 0, 0, tiled=True)
    return jnp.sum(got.astype(jnp.float32), axis=0)


def gather_rows(block, axis, n):
    rows, cols = block.shape
    got = lax.all_to_all(jnp.broadcast_to(block[None], (n, rows, cols)), axis, 0, 0, tiled=True)
    return got.reshape(n * rows, cols)


def reduce_dealt(part, pick, blocks):
    cols = part.shape[1]
    contract_rows = (((0,), (0,)), ((), ()))
    send = lax.dot_general(pick, part.astype(jnp.bfloat16), contract_rows, preferred_element_type=jnp.float32)
    send = send.astype(jnp.bfloat16).reshape(blocks, 2, -1, cols)
    odd = lax.axis_index("fsdp") % 2 == 1
    keep = jnp.where(odd, send[:, 1], send[:, 0])
    give = jnp.where(odd, send[:, 0], send[:, 1])
    got = lax.ppermute(give, "fsdp", [(f, f ^ 1) for f in range(blocks)])
    pair = (keep.astype(jnp.float32) + got.astype(jnp.float32)).astype(jnp.bfloat16)
    came = lax.all_to_all(pair, "fsdp", 0, 0, tiled=True)
    halves = jnp.sum(came.astype(jnp.float32).reshape(blocks // 2, 2, -1, cols), axis=0)
    return halves.reshape(-1, cols).astype(jnp.bfloat16)


def per_device(n_dp, n_fsdp, x_src, doc_lengths, doc_dests, w_gate, w_up, w_down, basis, out_cotangent):
    hidden_width = w_gate.shape[1]
    tok = x_src.shape[0]
    recv = out_cotangent.shape[0]
    loads, firsts = deal_tables(doc_lengths, doc_dests)
    rows_of = token_rows(doc_lengths, doc_dests, loads, tok, recv)
    dealt_rows = jnp.arange(n_fsdp * recv, dtype=jnp.int32)
    pick = (rows_of[:, None] == dealt_rows[None, :]).astype(jnp.bfloat16)
    contract_rows = (((0,), (0,)), ((), ()))
    contract_cols = (((1,), (1,)), ((), ()))

    half_x = tok // 2
    half_dy = recv // 2
    halves = jnp.stack([
        jnp.concatenate([x_src[:half_x], out_cotangent[:half_dy]], axis=0),
        jnp.concatenate([x_src[half_x:], out_cotangent[half_dy:]], axis=0),
    ])
    came = lax.all_to_all(jnp.tile(halves, (n_fsdp // 2, 1, 1)), "fsdp", 0, 0, tiled=True)
    other = lax.ppermute(came, "fsdp", [(f, f ^ 1) for f in range(n_fsdp)])
    odd = lax.axis_index("fsdp") % 2 == 1
    low = jnp.where(odd, other, came)
    high = jnp.where(odd, came, other)
    xall = jnp.concatenate([low[:, :half_x], high[:, :half_x]], axis=1).reshape(-1, x_src.shape[1])
    dy_dealt = jnp.concatenate([low[:, half_x:], high[:, half_x:]], axis=1).reshape(-1, x_src.shape[1])
    x_came = came[:, :half_x].reshape(-1, x_src.shape[1])
    x_other = other[:, :half_x].reshape(-1, x_src.shape[1])
    dyall = jnp.dot(pick, dy_dealt, preferred_element_type=jnp.float32).astype(jnp.bfloat16)
    key_half = basis.shape[1] // 2
    basis_half = lax.dynamic_slice_in_dim(basis, (lax.axis_index("fsdp") % 2) * key_half, key_half, 1)
    w_in = jnp.concatenate([w_gate, w_up, basis_half.astype(jnp.bfloat16)], axis=1)
    p_came = jnp.dot(x_came, w_in, preferred_element_type=jnp.float32).astype(jnp.bfloat16)
    p_other = jnp.dot(x_other, w_in, preferred_element_type=jnp.float32).astype(jnp.bfloat16)
    p_came = p_came.reshape(n_fsdp, half_x, -1)
    p_other = p_other.reshape(n_fsdp, half_x, -1)
    p_low = jnp.where(odd, p_other, p_came)
    p_high = jnp.where(odd, p_came, p_other)
    p_all = jnp.concatenate([p_low, p_high], axis=1).reshape(n_fsdp * tok, -1)
    first = p_all[:, :hidden_width]
    second = p_all[:, hidden_width:2 * hidden_width]
    keys_local = p_all[:, 2 * hidden_width:]
    hg_part = lax.dot_general(dyall, w_down, contract_cols, preferred_element_type=jnp.float32)
    both = reduce_rows(jnp.concatenate([first, second, keys_local, hg_part], axis=1), "dp", n_dp)
    gate = both[:, :hidden_width]
    up = both[:, hidden_width:2 * hidden_width]
    keys = both[:, 2 * hidden_width:2 * hidden_width + key_half].astype(jnp.bfloat16)
    hidden_grad = both[:, 2 * hidden_width + key_half:]
    sig = jax.nn.sigmoid(gate)
    hidden = (gate * sig * up).astype(jnp.bfloat16)

    gate_grad = (hidden_grad * up * sig * (1.0 + gate * (1.0 - sig))).astype(jnp.bfloat16)
    up_grad = (hidden_grad * gate * sig).astype(jnp.bfloat16)
    gathered = gather_rows(jnp.concatenate([hidden, gate_grad, up_grad, keys], axis=1), "dp", n_dp)
    hall = gathered[:, :hidden_width]
    gate_all = gathered[:, hidden_width:2 * hidden_width]
    up_all = gathered[:, 2 * hidden_width:3 * hidden_width]
    keys_mine = gathered[:, 3 * hidden_width:]
    keys_other = lax.ppermute(keys_mine, "fsdp", [(f, f ^ 1) for f in range(n_fsdp)])
    keys_all = jnp.where(
        odd,
        jnp.concatenate([keys_other, keys_mine], axis=1),
        jnp.concatenate([keys_mine, keys_other], axis=1),
    )
    out_part = jnp.dot(hall, w_down, preferred_element_type=jnp.float32)
    grad_down = lax.dot_general(hall, dyall, contract_rows, preferred_element_type=jnp.float32)
    total = lax.dot_general(gate_all, w_gate, contract_cols, preferred_element_type=jnp.float32)
    total = total + lax.dot_general(up_all, w_up, contract_cols, preferred_element_type=jnp.float32)
    model_width = out_part.shape[1]
    dealt = reduce_dealt(jnp.concatenate([out_part, total], axis=1), pick, n_fsdp)
    layer_out = dealt[:, :model_width]
    input_grad = dealt[:, model_width:]

    x_t = xall.T.astype(jnp.float32)
    keys_t = lax.dot_general(basis, keys_all, contract_cols, preferred_element_type=jnp.float32)
    xp_t = (x_t - keys_t).astype(jnp.bfloat16)
    grad_gate = jnp.dot(xp_t, gate_all, preferred_element_type=jnp.float32)
    grad_up = jnp.dot(xp_t, up_all, preferred_element_type=jnp.float32)
    return (layer_out, input_grad, grad_gate, grad_up, grad_down)


def solution(mesh):
    body = functools.partial(per_device, mesh.shape["dp"], mesh.shape["fsdp"])
    return jax.shard_map(
        body,
        mesh=mesh,
        in_specs=(
            P("fsdp", "dp"),
            P(),
            P(),
            P("dp", "fsdp"),
            P("dp", "fsdp"),
            P("fsdp", "dp"),
            P("dp", None),
            P("fsdp", "dp"),
        ),
        out_specs=(
            P("fsdp", "dp"),
            P("fsdp", "dp"),
            P("dp", "fsdp"),
            P("dp", "fsdp"),
            P("fsdp", "dp"),
        ),
        check_vma=False,
    )
```

```python
import functools

import jax
import jax.numpy as jnp
from jax import lax
from jax.sharding import PartitionSpec as P

MOST = 16


def deal_tables(doc_lengths, doc_dests):
    groups = doc_lengths.shape[0]
    starts = jnp.cumsum(doc_lengths, axis=1) - doc_lengths
    targets = jnp.arange(groups, dtype=jnp.int32)
    hits = (doc_dests[:, :, None] == targets[None, None, :]).astype(jnp.int32)
    loads = jnp.sum(doc_lengths[:, :, None] * hits, axis=1)
    firsts = jnp.sum(starts[:, :, None] * hits, axis=1)
    return (loads, firsts)


def token_rows(doc_lengths, doc_dests, loads, tok, recv):
    sources, ndoc = doc_lengths.shape
    starts = jnp.cumsum(doc_lengths, axis=1) - doc_lengths
    ends = starts + doc_lengths
    offsets = jnp.cumsum(loads, axis=0) - loads
    t = jnp.arange(tok, dtype=jnp.int32)
    doc_of = jnp.sum((ends[:, :, None] <= t[None, None, :]).astype(jnp.int32), axis=1)
    doc_of = jnp.minimum(doc_of, ndoc - 1)
    hit = (doc_of[:, :, None] == jnp.arange(ndoc, dtype=jnp.int32)[None, None, :]).astype(jnp.int32)
    dst = jnp.sum(hit * doc_dests[:, None, :], axis=2)
    st = jnp.sum(hit * starts[:, None, :], axis=2)
    to = (dst[:, :, None] == jnp.arange(sources, dtype=jnp.int32)[None, None, :]).astype(jnp.int32)
    off = jnp.sum(to * offsets[:, None, :], axis=2)
    row = dst * recv + off + t[None, :] - st
    return row.reshape(-1)


def settle(term):
    return lax.optimization_barrier(term.astype(jnp.bfloat16)).astype(jnp.float32)


def reduce_rows(part, axis, n):
    rows, cols = part.shape
    got = lax.all_to_all(part.astype(jnp.bfloat16).reshape(n, rows // n, cols), axis, 0, 0, tiled=True)
    return jnp.sum(got.astype(jnp.float32), axis=0)


def gather_rows(block, axis, n):
    rows, cols = block.shape
    got = lax.all_to_all(jnp.broadcast_to(block[None], (n, rows, cols)), axis, 0, 0, tiled=True)
    return got.reshape(n * rows, cols)


def pair_dealt(part, pick, blocks):
    cols = part.shape[1]
    contract_rows = (((0,), (0,)), ((), ()))
    send = lax.dot_general(pick, part.astype(jnp.bfloat16), contract_rows, preferred_element_type=jnp.float32)
    send = send.astype(jnp.bfloat16).reshape(blocks, 2, -1, cols)
    odd = lax.axis_index("fsdp") % 2 == 1
    keep = jnp.where(odd, send[:, 1], send[:, 0])
    give = jnp.where(odd, send[:, 0], send[:, 1])
    got = lax.ppermute(give, "fsdp", [(f, f ^ 1) for f in range(blocks)])
    return (keep.astype(jnp.float32) + got.astype(jnp.float32)).astype(jnp.bfloat16)


def reduce_dealt(pair, blocks):
    cols = pair.shape[2]
    came = lax.all_to_all(pair, "fsdp", 0, 0, tiled=True)
    halves = jnp.sum(came.astype(jnp.float32).reshape(blocks // 2, 2, -1, cols), axis=0)
    return halves.reshape(-1, cols).astype(jnp.bfloat16)


def per_device(n_dp, n_fsdp, x_src, doc_lengths, doc_dests, w_gate, w_up, w_down, basis, out_cotangent):
    hidden_width = w_gate.shape[1]
    tok = x_src.shape[0]
    recv = out_cotangent.shape[0]
    loads, firsts = deal_tables(doc_lengths, doc_dests)
    rows_of = token_rows(doc_lengths, doc_dests, loads, tok, recv)
    dealt_rows = jnp.arange(n_fsdp * recv, dtype=jnp.int32)
    pick = (rows_of[:, None] == dealt_rows[None, :]).astype(jnp.bfloat16)
    contract_rows = (((0,), (0,)), ((), ()))
    contract_cols = (((1,), (1,)), ((), ()))

    half_x = tok // 2
    half_dy = recv // 2
    halves = jnp.stack([
        jnp.concatenate([x_src[:half_x], out_cotangent[:half_dy]], axis=0),
        jnp.concatenate([x_src[half_x:], out_cotangent[half_dy:]], axis=0),
    ])
    came = lax.all_to_all(jnp.tile(halves, (n_fsdp // 2, 1, 1)), "fsdp", 0, 0, tiled=True)
    other = lax.ppermute(came, "fsdp", [(f, f ^ 1) for f in range(n_fsdp)])
    odd = lax.axis_index("fsdp") % 2 == 1
    low = jnp.where(odd, other, came)
    high = jnp.where(odd, came, other)
    xall = jnp.concatenate([low[:, :half_x], high[:, :half_x]], axis=1).reshape(-1, x_src.shape[1])
    dy_dealt = jnp.concatenate([low[:, half_x:], high[:, half_x:]], axis=1).reshape(-1, x_src.shape[1])
    dyall = jnp.dot(pick, dy_dealt, preferred_element_type=jnp.float32).astype(jnp.bfloat16)
    first = jnp.dot(xall, w_gate, preferred_element_type=jnp.float32)
    second = jnp.dot(xall, w_up, preferred_element_type=jnp.float32)
    key_half = basis.shape[1] // 2
    basis_half = lax.dynamic_slice_in_dim(basis, (lax.axis_index("fsdp") % 2) * key_half, key_half, 1)
    keys_local = jnp.dot(xall, basis_half, preferred_element_type=jnp.float32)
    hg_part = lax.dot_general(dyall, w_down, contract_cols, preferred_element_type=jnp.float32)
    both = reduce_rows(jnp.concatenate([first, second, keys_local, hg_part], axis=1), "dp", n_dp)
    gate = both[:, :hidden_width]
    up = both[:, hidden_width:2 * hidden_width]
    keys = both[:, 2 * hidden_width:2 * hidden_width + key_half].astype(jnp.bfloat16)
    hidden_grad = both[:, 2 * hidden_width + key_half:]
    sig = jax.nn.sigmoid(gate)
    hidden = (gate * sig * up).astype(jnp.bfloat16)

    gate_grad = (hidden_grad * up * sig * (1.0 + gate * (1.0 - sig))).astype(jnp.bfloat16)
    up_grad = (hidden_grad * gate * sig).astype(jnp.bfloat16)
    gathered = gather_rows(jnp.concatenate([hidden, gate_grad, up_grad, keys], axis=1), "dp", n_dp)
    hall = gathered[:, :hidden_width]
    gate_all = gathered[:, hidden_width:2 * hidden_width]
    up_all = gathered[:, 2 * hidden_width:3 * hidden_width]
    keys_mine = gathered[:, 3 * hidden_width:]
    keys_other = lax.ppermute(keys_mine, "fsdp", [(f, f ^ 1) for f in range(n_fsdp)])
    keys_all = jnp.where(
        odd,
        jnp.concatenate([keys_other, keys_mine], axis=1),
        jnp.concatenate([keys_mine, keys_other], axis=1),
    )
    out_part = jnp.dot(hall, w_down, preferred_element_type=jnp.float32)
    grad_down = lax.dot_general(hall, dyall, contract_rows, preferred_element_type=jnp.float32)
    total = lax.dot_general(gate_all, w_gate, contract_cols, preferred_element_type=jnp.float32)
    total = total + lax.dot_general(up_all, w_up, contract_cols, preferred_element_type=jnp.float32)
    model_width = out_part.shape[1]
    pairs = jnp.concatenate([pair_dealt(out_part, pick, n_fsdp), pair_dealt(total, pick, n_fsdp)], axis=2)
    dealt = reduce_dealt(pairs, n_fsdp)
    layer_out = dealt[:, :model_width]
    input_grad = dealt[:, model_width:]

    x_t = xall.T.astype(jnp.float32)
    keys_t = lax.dot_general(basis, keys_all, contract_cols, preferred_element_type=jnp.float32)
    xp_t = (x_t - keys_t).astype(jnp.bfloat16)
    grad_gate = jnp.dot(xp_t, gate_all, preferred_element_type=jnp.float32)
    grad_up = jnp.dot(xp_t, up_all, preferred_element_type=jnp.float32)
    return (layer_out, input_grad, grad_gate, grad_up, grad_down)


def solution(mesh):
    body = functools.partial(per_device, mesh.shape["dp"], mesh.shape["fsdp"])
    return jax.shard_map(
        body,
        mesh=mesh,
        in_specs=(
            P("fsdp", "dp"),
            P(),
            P(),
            P("dp", "fsdp"),
            P("dp", "fsdp"),
            P("fsdp", "dp"),
            P("dp", None),
            P("fsdp", "dp"),
        ),
        out_specs=(
            P("fsdp", "dp"),
            P("fsdp", "dp"),
            P("dp", "fsdp"),
            P("dp", "fsdp"),
            P("fsdp", "dp"),
        ),
        check_vma=False,
    )
```

```python
import functools

import jax
import jax.numpy as jnp
from jax import lax
from jax.sharding import PartitionSpec as P

MOST = 16


def deal_tables(doc_lengths, doc_dests):
    groups = doc_lengths.shape[0]
    starts = jnp.cumsum(doc_lengths, axis=1) - doc_lengths
    targets = jnp.arange(groups, dtype=jnp.int32)
    hits = (doc_dests[:, :, None] == targets[None, None, :]).astype(jnp.int32)
    loads = jnp.sum(doc_lengths[:, :, None] * hits, axis=1)
    firsts = jnp.sum(starts[:, :, None] * hits, axis=1)
    return (loads, firsts)


def token_rows(doc_lengths, doc_dests, loads, tok, recv):
    sources, ndoc = doc_lengths.shape
    starts = jnp.cumsum(doc_lengths, axis=1) - doc_lengths
    ends = starts + doc_lengths
    offsets = jnp.cumsum(loads, axis=0) - loads
    t = jnp.arange(tok, dtype=jnp.int32)
    doc_of = jnp.sum((ends[:, :, None] <= t[None, None, :]).astype(jnp.int32), axis=1)
    doc_of = jnp.minimum(doc_of, ndoc - 1)
    hit = (doc_of[:, :, None] == jnp.arange(ndoc, dtype=jnp.int32)[None, None, :]).astype(jnp.int32)
    dst = jnp.sum(hit * doc_dests[:, None, :], axis=2)
    st = jnp.sum(hit * starts[:, None, :], axis=2)
    to = (dst[:, :, None] == jnp.arange(sources, dtype=jnp.int32)[None, None, :]).astype(jnp.int32)
    off = jnp.sum(to * offsets[:, None, :], axis=2)
    row = dst * recv + off + t[None, :] - st
    return row.reshape(-1)


def settle(term):
    return lax.optimization_barrier(term.astype(jnp.bfloat16)).astype(jnp.float32)


def reduce_rows(part, axis, n):
    rows, cols = part.shape
    got = lax.all_to_all(part.astype(jnp.bfloat16).reshape(n, rows // n, cols), axis, 0, 0, tiled=True)
    return jnp.sum(got.astype(jnp.float32), axis=0)


def gather_rows(block, axis, n):
    rows, cols = block.shape
    got = lax.all_to_all(jnp.broadcast_to(block[None], (n, rows, cols)), axis, 0, 0, tiled=True)
    return got.reshape(n * rows, cols)


def reduce_dealt(part, pick, blocks):
    cols = part.shape[1]
    contract_rows = (((0,), (0,)), ((), ()))
    send = lax.dot_general(pick, part.astype(jnp.bfloat16), contract_rows, preferred_element_type=jnp.float32)
    send = send.astype(jnp.bfloat16).reshape(blocks, 2, -1, cols)
    odd = lax.axis_index("fsdp") % 2 == 1
    keep = jnp.where(odd, send[:, 1], send[:, 0])
    give = jnp.where(odd, send[:, 0], send[:, 1])
    got = lax.ppermute(give, "fsdp", [(f, f ^ 1) for f in range(blocks)])
    pair = (keep.astype(jnp.float32) + got.astype(jnp.float32)).astype(jnp.bfloat16)
    came = lax.all_to_all(pair, "fsdp", 0, 0, tiled=True)
    halves = jnp.sum(came.astype(jnp.float32).reshape(blocks // 2, 2, -1, cols), axis=0)
    return halves.reshape(-1, cols).astype(jnp.bfloat16)


def per_device(n_dp, n_fsdp, x_src, doc_lengths, doc_dests, w_gate, w_up, w_down, basis, out_cotangent):
    hidden_width = w_gate.shape[1]
    tok = x_src.shape[0]
    recv = out_cotangent.shape[0]
    loads, firsts = deal_tables(doc_lengths, doc_dests)
    rows_of = token_rows(doc_lengths, doc_dests, loads, tok, recv)
    dealt_rows = jnp.arange(n_fsdp * recv, dtype=jnp.int32)
    contract_rows = (((0,), (0,)), ((), ()))
    contract_cols = (((1,), (1,)), ((), ()))

    half_x = tok // 2
    half_dy = recv // 2
    halves = jnp.stack([
        jnp.concatenate([x_src[:half_x], out_cotangent[:half_dy]], axis=0),
        jnp.concatenate([x_src[half_x:], out_cotangent[half_dy:]], axis=0),
    ])
    came = lax.all_to_all(jnp.tile(halves, (n_fsdp // 2, 1, 1)), "fsdp", 0, 0, tiled=True)
    other = lax.ppermute(came, "fsdp", [(f, f ^ 1) for f in range(n_fsdp)])
    odd = lax.axis_index("fsdp") % 2 == 1
    parity = lax.axis_index("fsdp") % 2
    width = x_src.shape[1]
    xall = jnp.concatenate([came[:, :half_x].reshape(-1, width), other[:, :half_x].reshape(-1, width)])
    dy_rows = jnp.concatenate([came[:, half_x:].reshape(-1, width), other[:, half_x:].reshape(-1, width)])
    rows3 = rows_of.reshape(n_fsdp, 2, half_x)
    mine = jnp.where(odd, rows3[:, 1], rows3[:, 0])
    theirs = jnp.where(odd, rows3[:, 0], rows3[:, 1])
    rows_perm = jnp.concatenate([mine.reshape(-1), theirs.reshape(-1)])
    pick = (rows_perm[:, None] == dealt_rows[None, :]).astype(jnp.bfloat16)
    src_i = jnp.arange(n_fsdp, dtype=jnp.int32)[:, None] * recv
    within = jnp.arange(half_dy, dtype=jnp.int32)[None, :]
    label = jnp.concatenate([
        (src_i + parity * half_dy + within).reshape(-1),
        (src_i + (1 - parity) * half_dy + within).reshape(-1),
    ])
    pick_dy = (rows_perm[:, None] == label[None, :]).astype(jnp.bfloat16)
    dyall = jnp.dot(pick_dy, dy_rows, preferred_element_type=jnp.float32).astype(jnp.bfloat16)
    first = jnp.dot(xall, w_gate, preferred_element_type=jnp.float32)
    second = jnp.dot(xall, w_up, preferred_element_type=jnp.float32)
    key_half = basis.shape[1] // 2
    basis_half = lax.dynamic_slice_in_dim(basis, (lax.axis_index("fsdp") % 2) * key_half, key_half, 1)
    keys_local = jnp.dot(xall, basis_half, preferred_element_type=jnp.float32)
    hg_part = lax.dot_general(dyall, w_down, contract_cols, preferred_element_type=jnp.float32)
    both = reduce_rows(jnp.concatenate([first, second, keys_local, hg_part], axis=1), "dp", n_dp)
    gate = both[:, :hidden_width]
    up = both[:, hidden_width:2 * hidden_width]
    keys = both[:, 2 * hidden_width:2 * hidden_width + key_half].astype(jnp.bfloat16)
    hidden_grad = both[:, 2 * hidden_width + key_half:]
    sig = jax.nn.sigmoid(gate)
    hidden = (gate * sig * up).astype(jnp.bfloat16)

    gate_grad = (hidden_grad * up * sig * (1.0 + gate * (1.0 - sig))).astype(jnp.bfloat16)
    up_grad = (hidden_grad * gate * sig).astype(jnp.bfloat16)
    gathered = gather_rows(jnp.concatenate([hidden, gate_grad, up_grad, keys], axis=1), "dp", n_dp)
    hall = gathered[:, :hidden_width]
    gate_all = gathered[:, hidden_width:2 * hidden_width]
    up_all = gathered[:, 2 * hidden_width:3 * hidden_width]
    keys_mine = gathered[:, 3 * hidden_width:]
    keys_other = lax.ppermute(keys_mine, "fsdp", [(f, f ^ 1) for f in range(n_fsdp)])
    rows_half = keys_other.shape[0] // 2
    keys_other = jnp.concatenate([keys_other[rows_half:], keys_other[:rows_half]])
    keys_all = jnp.where(
        odd,
        jnp.concatenate([keys_other, keys_mine], axis=1),
        jnp.concatenate([keys_mine, keys_other], axis=1),
    )
    out_part = jnp.dot(hall, w_down, preferred_element_type=jnp.float32)
    grad_down = lax.dot_general(hall, dyall, contract_rows, preferred_element_type=jnp.float32)
    total = lax.dot_general(gate_all, w_gate, contract_cols, preferred_element_type=jnp.float32)
    total = total + lax.dot_general(up_all, w_up, contract_cols, preferred_element_type=jnp.float32)
    model_width = out_part.shape[1]
    dealt = reduce_dealt(jnp.concatenate([out_part, total], axis=1), pick, n_fsdp)
    layer_out = dealt[:, :model_width]
    input_grad = dealt[:, model_width:]

    x_t = xall.T.astype(jnp.float32)
    keys_t = lax.dot_general(basis, keys_all, contract_cols, preferred_element_type=jnp.float32)
    xp_t = (x_t - keys_t).astype(jnp.bfloat16)
    grad_gate = jnp.dot(xp_t, gate_all, preferred_element_type=jnp.float32)
    grad_up = jnp.dot(xp_t, up_all, preferred_element_type=jnp.float32)
    return (layer_out, input_grad, grad_gate, grad_up, grad_down)


def solution(mesh):
    body = functools.partial(per_device, mesh.shape["dp"], mesh.shape["fsdp"])
    return jax.shard_map(
        body,
        mesh=mesh,
        in_specs=(
            P("fsdp", "dp"),
            P(),
            P(),
            P("dp", "fsdp"),
            P("dp", "fsdp"),
            P("fsdp", "dp"),
            P("dp", None),
            P("fsdp", "dp"),
        ),
        out_specs=(
            P("fsdp", "dp"),
            P("fsdp", "dp"),
            P("dp", "fsdp"),
            P("dp", "fsdp"),
            P("fsdp", "dp"),
        ),
        check_vma=False,
    )
```
